512 devices in a mesh: shift: 4 (over x_hi, core), space: 128 (over y, z, x_lo).
Axes of the slice: x: 4 (x_hi: 2, x_lo: 2; x = x_hi * 2 + x_lo), y: 8, z: 8, core: 2. Of those that a mesh axis runs over, the one named last changes fastest.
Arguments:
- labels: int32 [256, 32, 256], P('space'), may hold values from 0 to 7
- conductance: float32 [8], replicated, may hold values from 0.2 to 5
- capacity_table: float32 [8], replicated, may hold values from 0.5 to 2
- shift_values: float32 [8], replicated, may hold values from 0.1 to 4
- prior_basis: float32 [256, 256, 32, 256], P(None, 'space', 'shift'), may hold values from -6 to 6
Outputs:
- new_block: float32 [8, 8, 256, 32, 256], P(None, None, 'space', 'shift')
- coefficients: float32 [64, 256], replicated
- factor: float32 [64, 64], replicated
The draws below stay inside these ranges and needn't reach their ends.
All inputs are finite; a program needn't handle non-finite values.
Results may differ from the reference program's by a relative error of at most 0.0003.
Values sent between devices are 32-bit elements; how exact they have to be, the bound alone decides.
No kernel may reach another device: no remote copies, remote signals or barrier semaphores. Data moves between devices by JAX's collectives and lax.ppermute only.
A program may use at most 64 MiB of HBM per device.

```python
import math
import jax
import jax.numpy as jnp
from jax import lax

NY = 32
NZ = 256
COLS = 8
BASIS = 256
SWEEPS = 4
MATS = 8
SHIFTS = 8
NEW = 64
NX = 256


def draw_basis_values(key):
    first_key, second_key, third_key = jax.random.split(jax.random.fold_in(key, 17), 3)
    scales = jnp.exp(jax.random.uniform(first_key, (BASIS, 1), jnp.float32, jnp.log(0.6), jnp.log(1.5)))
    values = jax.random.truncated_normal(second_key, -4.0, 4.0, (BASIS, NX * NY * NZ), jnp.float32)
    mixing = jnp.eye(BASIS, dtype=jnp.float32) + 0.5 * BASIS ** (-0.5) * jax.random.normal(third_key, (BASIS, BASIS), jnp.float32)
    mixed = jnp.dot(mixing, values, precision=lax.Precision.HIGHEST) * scales
    return jnp.clip(mixed, -6.0, 6.0).reshape(BASIS, NX, NY, NZ)


def draw_prior_basis(key, part):
    return draw_basis_values(key)


def plant(array, own_key, least, high):
    longest = array.shape.index(max(array.shape))
    spots = []
    for shift in (0, 1):
        where = [jax.random.randint(jax.random.fold_in(own_key, axis), (), 0, length) for axis, length in enumerate(array.shape)]
        where[longest] = (where[longest] + shift) % array.shape[longest]
        spots.append(tuple(where))
    return array.at[spots[0]].set(least).at[spots[1]].set(high)


def setup_inputs(seed: int = 0) -> dict:
    seeds = jax.random.split(jax.random.key(seed), 6)
    return {
        "labels": plant(jax.random.randint(seeds[0], (NX, NY, NZ), 0, MATS), jax.random.fold_in(seeds[0], 1), 0, MATS - 1).astype(jnp.int32),
        "conductance": jnp.clip(jnp.exp(jax.random.uniform(seeds[1], (MATS,), jnp.float32, math.log(0.2), math.log(5.0))), 0.2, 5.0),
        "capacity_table": jnp.clip(jnp.exp(jax.random.uniform(seeds[2], (MATS,), jnp.float32, math.log(0.5), math.log(2.0))), 0.5, 2.0),
        "shift_values": jnp.clip(jnp.exp(jax.random.uniform(seeds[3], (SHIFTS,), jnp.float32, math.log(0.1), math.log(4.0))), 0.1, 4.0),
        "prior_basis": draw_prior_basis(jax.random.fold_in(seeds[5], 71), 0),
    }


LOWER_BOUND = 0.1
UPPER_BOUND = 2.0

def conductances(conduct, padded):
    west_face = 0.5 * (conduct + padded[:-2, 1:-1, 1:-1])
    east_face = 0.5 * (conduct + padded[2:, 1:-1, 1:-1])
    south_face = 0.5 * (conduct + padded[1:-1, :-2, 1:-1])
    north_face = 0.5 * (conduct + padded[1:-1, 2:, 1:-1])
    below_face = 0.5 * (conduct + padded[1:-1, 1:-1, :-2])
    above_face = 0.5 * (conduct + padded[1:-1, 1:-1, 2:])
    return (west_face, east_face, south_face, north_face, below_face, above_face)

def neighbours(padded, face_list):
    west_face, east_face, south_face, north_face, below_face, above_face = face_list
    summed = west_face * padded[..., :-2, 1:-1, 1:-1] + east_face * padded[..., 2:, 1:-1, 1:-1]
    summed = summed + south_face * padded[..., 1:-1, :-2, 1:-1] + north_face * padded[..., 1:-1, 2:, 1:-1]
    summed = summed + below_face * padded[..., 1:-1, 1:-1, :-2] + above_face * padded[..., 1:-1, 1:-1, 2:]
    return summed

def chebyshev(source, face_list, diagonal, padder):
    center = 0.5 * (UPPER_BOUND + LOWER_BOUND)
    spread = 0.5 * (UPPER_BOUND - LOWER_BOUND)
    ratio_value = center / spread
    reciprocal = 1.0 / diagonal
    solution = jnp.zeros_like(source)
    remainder = source
    weight_old = 1.0 / ratio_value
    direction = reciprocal * remainder / center
    for sweep_index in range(SWEEPS):
        solution = solution + direction
        if sweep_index + 1 < SWEEPS:
            applied = diagonal * direction - neighbours(padder(direction), face_list)
            remainder = remainder - applied
            weight_new = 1.0 / (2.0 * ratio_value - weight_old)
            direction = weight_new * weight_old * direction + 2.0 * weight_new / spread * (reciprocal * remainder)
            weight_old = weight_new
    return solution

def products(left_side, right_side):
    return lax.dot_general(left_side, right_side, (((1,), (1,)), ((), ())), precision=lax.Precision.HIGHEST)

def reference(labels, conductance, capacity_table, shift_values, prior_basis):
    conduct = conductance[labels]
    capacity = capacity_table[labels]
    face_list = conductances(conduct, jnp.pad(conduct, 1))
    west_face, east_face, south_face, north_face, below_face, above_face = face_list
    summed = west_face + east_face + (south_face + north_face) + (below_face + above_face)
    diagonal = summed[None, None] + shift_values[:, None, None, None, None] * capacity[None, None]
    tail_columns = prior_basis[BASIS - NEW:].reshape(SHIFTS, COLS, NX, NY, NZ)
    source = tail_columns * capacity[None, None]

    def padder(field):
        return jnp.pad(field, ((0, 0), (0, 0), (1, 1), (1, 1), (1, 1)))
    fields = chebyshev(source, face_list, diagonal, padder)
    cell_weight = 1.0 / (NX * NY * NZ)
    columns = fields.reshape(NEW, NX * NY * NZ)
    flat_basis = prior_basis.reshape(BASIS, NX * NY * NZ)
    first_proj = products(columns, flat_basis) * cell_weight
    columns = columns - jnp.dot(first_proj, flat_basis, precision=lax.Precision.HIGHEST)
    second_proj = products(columns, flat_basis) * cell_weight
    columns = columns - jnp.dot(second_proj, flat_basis, precision=lax.Precision.HIGHEST)
    gram_matrix = products(columns, columns) * cell_weight
    factor = jnp.linalg.cholesky(gram_matrix)
    orthonormal = lax.linalg.triangular_solve(factor, columns, left_side=True, lower=True)
    return (orthonormal.reshape(SHIFTS, COLS, NX, NY, NZ), first_proj + second_proj, factor)
```

```python
import jax
import jax.numpy as jnp
from jax import lax
from jax.sharding import PartitionSpec as P

COLS = 8
SWEEPS = 4


LOWER_BOUND = 0.1
UPPER_BOUND = 2.0


def padded_2(cells, sides, width):
    for axis, dim in sides:
        count = lax.axis_size(axis)
        ends = count - 1
        head = lax.slice_in_dim(cells, 0, width, axis=dim)
        tail = lax.slice_in_dim(cells, cells.shape[dim] - width, cells.shape[dim], axis=dim)
        cells = jnp.concatenate(
            [
                lax.ppermute(tail, axis, [(i, (i + 1) % count) for i in range(ends)]),
                cells,
                lax.ppermute(head, axis, [((i + 1) % count, i) for i in range(ends)]),
            ],
            axis=dim,
        )
    return cells


def allsum(value):
    axes = ("shift", "space")
    total = lax.axis_size("shift") * lax.axis_size("space")
    if total & (total - 1):
        return lax.psum(value, axes)
    for bit in range(total.bit_length() - 1):
        mask = 1 << bit
        value = value + lax.ppermute(value, axes, [(i, i ^ mask) for i in range(total)])
    return value


def lookup(labels, table):
    materials = jnp.arange(table.shape[0], dtype=jnp.int32)
    onehot = (labels[None] == materials[:, None, None, None]).astype(jnp.float32)
    return jnp.sum(onehot * table[:, None, None, None], axis=0)


def conductances(conduct, padded):
    west_face = 0.5 * (conduct + padded[:-2, 1:-1, 1:-1])
    east_face = 0.5 * (conduct + padded[2:, 1:-1, 1:-1])
    south_face = 0.5 * (conduct + padded[1:-1, :-2, 1:-1])
    north_face = 0.5 * (conduct + padded[1:-1, 2:, 1:-1])
    below_face = 0.5 * (conduct + padded[1:-1, 1:-1, :-2])
    above_face = 0.5 * (conduct + padded[1:-1, 1:-1, 2:])
    return (west_face, east_face, south_face, north_face, below_face, above_face)


def neighbours(padded, face_list):
    west_face, east_face, south_face, north_face, below_face, above_face = face_list
    summed = west_face * padded[..., :-2, 1:-1, 1:-1] + east_face * padded[..., 2:, 1:-1, 1:-1]
    summed = (
        summed
        + south_face * padded[..., 1:-1, :-2, 1:-1]
        + north_face * padded[..., 1:-1, 2:, 1:-1]
    )
    summed = (
        summed
        + below_face * padded[..., 1:-1, 1:-1, :-2]
        + above_face * padded[..., 1:-1, 1:-1, 2:]
    )
    return summed


def diagonal_of(face_list, shift_list, capacity):
    west_face, east_face, south_face, north_face, below_face, above_face = face_list
    summed = west_face + east_face + (south_face + north_face) + (below_face + above_face)
    return summed[None, None] + shift_list[:, None, None, None, None] * capacity[None, None]


def chebyshev(source, face_list, diagonal, padder):
    center = 0.5 * (UPPER_BOUND + LOWER_BOUND)
    spread = 0.5 * (UPPER_BOUND - LOWER_BOUND)
    ratio_value = center / spread
    reciprocal = 1.0 / diagonal
    solution = jnp.zeros_like(source)
    remainder = source
    weight_old = 1.0 / ratio_value
    direction = reciprocal * remainder / center
    for sweep_index in range(SWEEPS):
        solution = solution + direction
        if sweep_index + 1 < SWEEPS:
            applied = diagonal * direction - neighbours(padder(direction), face_list)
            remainder = remainder - applied
            weight_new = 1.0 / (2.0 * ratio_value - weight_old)
            direction = weight_new * weight_old * direction + 2.0 * weight_new / spread * (
                reciprocal * remainder
            )
            weight_old = weight_new
    return solution


def products(left_side, right_side):
    return lax.dot_general(
        left_side, right_side, (((1,), (1,)), ((), ())), precision=lax.Precision.HIGHEST
    )


def matmul(left_side, right_side):
    return jnp.dot(left_side, right_side, precision=lax.Precision.HIGHEST)


def local(labels, conductance, capacity_table, shift_values, prior_basis):
    groups = lax.axis_size("shift")
    shifts_all = shift_values.shape[0]
    per_device = shifts_all // groups
    new_count = shifts_all * COLS
    basis_count = prior_basis.shape[0]
    slab_x = prior_basis.shape[1]
    quarter = prior_basis.shape[2]
    depth = prior_basis.shape[3]
    flat_basis = prior_basis.reshape(basis_count, slab_x * quarter * depth)
    cell_weight = 1.0 / (slab_x * quarter * depth * groups * lax.axis_size("space"))
    tail_columns = prior_basis[basis_count - new_count :]
    conduct = lookup(labels, conductance)
    capacity = lookup(labels, capacity_table)
    rimmed = padded_2(conduct, (("space", 0),), 1)
    face_list = conductances(conduct, jnp.pad(rimmed, ((0, 0), (1, 1), (1, 1))))
    shift_list = lax.dynamic_slice_in_dim(
        shift_values, lax.axis_index("shift") * per_device, per_device, 0
    )
    diagonal = diagonal_of(face_list, shift_list, capacity)
    starting = lax.all_to_all(tail_columns, "shift", split_axis=0, concat_axis=2, tiled=True)
    full_y = starting.shape[2]
    source = starting.reshape(per_device, COLS, slab_x, full_y, depth) * capacity[None, None]

    def padder(field):
        widened = padded_2(field, (("space", 2),), 1)
        return jnp.pad(widened, ((0, 0), (0, 0), (0, 0), (1, 1), (1, 1)))

    fields = chebyshev(source, face_list, diagonal, padder)
    merged = fields.reshape(per_device * COLS, slab_x, full_y, depth)
    regrouped = lax.all_to_all(merged, "shift", split_axis=2, concat_axis=0, tiled=True)
    columns = regrouped.reshape(new_count, slab_x * quarter * depth)
    first_proj = allsum(products(columns, flat_basis)) * cell_weight
    columns = columns - matmul(first_proj, flat_basis)
    second_proj = allsum(products(columns, flat_basis)) * cell_weight
    columns = columns - matmul(second_proj, flat_basis)
    gram_matrix = allsum(products(columns, columns)) * cell_weight
    factor = jnp.linalg.cholesky(gram_matrix)
    orthonormal = lax.linalg.triangular_solve(factor, columns, left_side=True, lower=True)
    new_block = orthonormal.reshape(shifts_all, COLS, slab_x, quarter, depth)
    return (new_block, first_proj + second_proj, factor)


def solution(mesh):
    in_specs = (P("space", None, None), P(), P(), P(), P(None, "space", "shift", None))
    out_specs = (P(None, None, "space", "shift", None), P(), P())
    return jax.shard_map(local, mesh=mesh, in_specs=in_specs, out_specs=out_specs, check_vma=False)
```

```python
import jax
import jax.numpy as jnp
from jax import lax
from jax.sharding import PartitionSpec as P

COLS = 8
SWEEPS = 4


LOWER_BOUND = 0.1
UPPER_BOUND = 2.0


def padded_2(cells, sides, width):
    for axis, dim in sides:
        count = lax.axis_size(axis)
        ends = count - 1
        head = lax.slice_in_dim(cells, 0, width, axis=dim)
        tail = lax.slice_in_dim(cells, cells.shape[dim] - width, cells.shape[dim], axis=dim)
        cells = jnp.concatenate(
            [
                lax.ppermute(tail, axis, [(i, (i + 1) % count) for i in range(ends)]),
                cells,
                lax.ppermute(head, axis, [((i + 1) % count, i) for i in range(ends)]),
            ],
            axis=dim,
        )
    return cells


def allsum(value):
    axes = ("shift", "space")
    total = lax.axis_size("shift") * lax.axis_size("space")
    if total & (total - 1):
        return lax.psum(value, axes)
    for bit in range(total.bit_length() - 1):
        mask = 1 << bit
        value = value + lax.ppermute(value, axes, [(i, i ^ mask) for i in range(total)])
    return value


def lookup(labels, table):
    materials = jnp.arange(table.shape[0], dtype=jnp.int32)
    onehot = (labels[None] == materials[:, None, None, None]).astype(jnp.float32)
    return jnp.sum(onehot * table[:, None, None, None], axis=0)


def conductances(conduct, padded):
    west_face = 0.5 * (conduct + padded[:-2, 1:-1, 1:-1])
    east_face = 0.5 * (conduct + padded[2:, 1:-1, 1:-1])
    south_face = 0.5 * (conduct + padded[1:-1, :-2, 1:-1])
    north_face = 0.5 * (conduct + padded[1:-1, 2:, 1:-1])
    below_face = 0.5 * (conduct + padded[1:-1, 1:-1, :-2])
    above_face = 0.5 * (conduct + padded[1:-1, 1:-1, 2:])
    return (west_face, east_face, south_face, north_face, below_face, above_face)


def neighbours(padded, face_list):
    west_face, east_face, south_face, north_face, below_face, above_face = face_list
    summed = west_face * padded[..., :-2, 1:-1, 1:-1] + east_face * padded[..., 2:, 1:-1, 1:-1]
    summed = (
        summed
        + south_face * padded[..., 1:-1, :-2, 1:-1]
        + north_face * padded[..., 1:-1, 2:, 1:-1]
    )
    summed = (
        summed
        + below_face * padded[..., 1:-1, 1:-1, :-2]
        + above_face * padded[..., 1:-1, 1:-1, 2:]
    )
    return summed


def diagonal_of(face_list, shift_list, capacity):
    west_face, east_face, south_face, north_face, below_face, above_face = face_list
    summed = west_face + east_face + (south_face + north_face) + (below_face + above_face)
    return summed[None, None] + shift_list[:, None, None, None, None] * capacity[None, None]


def chebyshev(source, face_list, diagonal, padder):
    center = 0.5 * (UPPER_BOUND + LOWER_BOUND)
    spread = 0.5 * (UPPER_BOUND - LOWER_BOUND)
    ratio_value = center / spread
    reciprocal = 1.0 / diagonal
    solution = jnp.zeros_like(source)
    remainder = source
    weight_old = 1.0 / ratio_value
    direction = reciprocal * remainder / center
    for sweep_index in range(SWEEPS):
        solution = solution + direction
        if sweep_index + 1 < SWEEPS:
            applied = diagonal * direction - neighbours(padder(direction), face_list)
            remainder = remainder - applied
            weight_new = 1.0 / (2.0 * ratio_value - weight_old)
            direction = weight_new * weight_old * direction + 2.0 * weight_new / spread * (
                reciprocal * remainder
            )
            weight_old = weight_new
    return solution


def products(left_side, right_side):
    return lax.dot_general(
        left_side, right_side, (((1,), (1,)), ((), ())), precision=lax.Precision.HIGHEST
    )


def matmul(left_side, right_side):
    return jnp.dot(left_side, right_side, precision=lax.Precision.HIGHEST)


def local(labels, conductance, capacity_table, shift_values, prior_basis):
    groups = lax.axis_size("shift")
    shifts_all = shift_values.shape[0]
    per_device = shifts_all // groups
    new_count = shifts_all * COLS
    basis_count = prior_basis.shape[0]
    slab_x = prior_basis.shape[1]
    quarter = prior_basis.shape[2]
    depth = prior_basis.shape[3]
    flat_basis = prior_basis.reshape(basis_count, slab_x * quarter * depth)
    cell_weight = 1.0 / (slab_x * quarter * depth * groups * lax.axis_size("space"))
    tail_columns = prior_basis[basis_count - new_count :]
    basis_gram = allsum(products(flat_basis, flat_basis)) * cell_weight
    conduct = lookup(labels, conductance)
    capacity = lookup(labels, capacity_table)
    rimmed = padded_2(conduct, (("space", 0),), 1)
    face_list = conductances(conduct, jnp.pad(rimmed, ((0, 0), (1, 1), (1, 1))))
    shift_list = lax.dynamic_slice_in_dim(
        shift_values, lax.axis_index("shift") * per_device, per_device, 0
    )
    diagonal = diagonal_of(face_list, shift_list, capacity)
    starting = lax.all_to_all(tail_columns, "shift", split_axis=0, concat_axis=2, tiled=True)
    full_y = starting.shape[2]
    source = starting.reshape(per_device, COLS, slab_x, full_y, depth) * capacity[None, None]

    def padder(field):
        widened = padded_2(field, (("space", 2),), 1)
        return jnp.pad(widened, ((0, 0), (0, 0), (0, 0), (1, 1), (1, 1)))

    fields = chebyshev(source, face_list, diagonal, padder)
    merged = fields.reshape(per_device * COLS, slab_x, full_y, depth)
    regrouped = lax.all_to_all(merged, "shift", split_axis=2, concat_axis=0, tiled=True)
    columns = regrouped.reshape(new_count, slab_x * quarter * depth)
    first_proj = allsum(products(columns, flat_basis)) * cell_weight
    second_proj = first_proj - matmul(first_proj, basis_gram)
    columns = columns - matmul(first_proj + second_proj, flat_basis)
    gram_matrix = allsum(products(columns, columns)) * cell_weight
    factor = jnp.linalg.cholesky(gram_matrix)
    orthonormal = lax.linalg.triangular_solve(factor, columns, left_side=True, lower=True)
    new_block = orthonormal.reshape(shifts_all, COLS, slab_x, quarter, depth)
    return (new_block, first_proj + second_proj, factor)


def solution(mesh):
    in_specs = (P("space", None, None), P(), P(), P(), P(None, "space", "shift", None))
    out_specs = (P(None, None, "space", "shift", None), P(), P())
    return jax.shard_map(local, mesh=mesh, in_specs=in_specs, out_specs=out_specs, check_vma=False)
```

```python
import jax
import jax.numpy as jnp
from jax import lax
from jax.sharding import PartitionSpec as P

COLS = 8
SWEEPS = 4


LOWER_BOUND = 0.1
UPPER_BOUND = 2.0


def padded_2(cells, sides, width):
    for axis, dim in sides:
        count = lax.axis_size(axis)
        ends = count - 1
        head = lax.slice_in_dim(cells, 0, width, axis=dim)
        tail = lax.slice_in_dim(cells, cells.shape[dim] - width, cells.shape[dim], axis=dim)
        cells = jnp.concatenate(
            [
                lax.ppermute(tail, axis, [(i, (i + 1) % count) for i in range(ends)]),
                cells,
                lax.ppermute(head, axis, [((i + 1) % count, i) for i in range(ends)]),
            ],
            axis=dim,
        )
    return cells


def allsum(value):
    axes = ("shift", "space")
    total = lax.axis_size("shift") * lax.axis_size("space")
    if total & (total - 1):
        return lax.psum(value, axes)
    for bit in range(total.bit_length() - 1):
        mask = 1 << bit
        value = value + lax.ppermute(value, axes, [(i, i ^ mask) for i in range(total)])
    return value


def lookup(labels, table):
    materials = jnp.arange(table.shape[0], dtype=jnp.int32)
    onehot = (labels[None] == materials[:, None, None, None]).astype(jnp.float32)
    return jnp.sum(onehot * table[:, None, None, None], axis=0)


def conductances(conduct, padded):
    west_face = 0.5 * (conduct + padded[:-2, 1:-1, 1:-1])
    east_face = 0.5 * (conduct + padded[2:, 1:-1, 1:-1])
    south_face = 0.5 * (conduct + padded[1:-1, :-2, 1:-1])
    north_face = 0.5 * (conduct + padded[1:-1, 2:, 1:-1])
    below_face = 0.5 * (conduct + padded[1:-1, 1:-1, :-2])
    above_face = 0.5 * (conduct + padded[1:-1, 1:-1, 2:])
    return (west_face, east_face, south_face, north_face, below_face, above_face)


def neighbours(padded, face_list):
    west_face, east_face, south_face, north_face, below_face, above_face = face_list
    summed = west_face * padded[..., :-2, 1:-1, 1:-1] + east_face * padded[..., 2:, 1:-1, 1:-1]
    summed = (
        summed
        + south_face * padded[..., 1:-1, :-2, 1:-1]
        + north_face * padded[..., 1:-1, 2:, 1:-1]
    )
    summed = (
        summed
        + below_face * padded[..., 1:-1, 1:-1, :-2]
        + above_face * padded[..., 1:-1, 1:-1, 2:]
    )
    return summed


def diagonal_of(face_list, shift_list, capacity):
    west_face, east_face, south_face, north_face, below_face, above_face = face_list
    summed = west_face + east_face + (south_face + north_face) + (below_face + above_face)
    return summed[None, None] + shift_list[:, None, None, None, None] * capacity[None, None]


def chebyshev(source, face_list, diagonal, padder):
    center = 0.5 * (UPPER_BOUND + LOWER_BOUND)
    spread = 0.5 * (UPPER_BOUND - LOWER_BOUND)
    ratio_value = center / spread
    reciprocal = 1.0 / diagonal
    solution = jnp.zeros_like(source)
    remainder = source
    weight_old = 1.0 / ratio_value
    direction = reciprocal * remainder / center
    for sweep_index in range(SWEEPS):
        solution = solution + direction
        if sweep_index + 1 < SWEEPS:
            applied = diagonal * direction - neighbours(padder(direction), face_list)
            remainder = remainder - applied
            weight_new = 1.0 / (2.0 * ratio_value - weight_old)
            direction = weight_new * weight_old * direction + 2.0 * weight_new / spread * (
                reciprocal * remainder
            )
            weight_old = weight_new
    return solution


def products(left_side, right_side):
    return lax.dot_general(
        left_side, right_side, (((1,), (1,)), ((), ())), precision=lax.Precision.HIGHEST
    )


def matmul(left_side, right_side):
    return jnp.dot(left_side, right_side, precision=lax.Precision.HIGHEST)


def local(labels, conductance, capacity_table, shift_values, prior_basis):
    groups = lax.axis_size("shift")
    shifts_all = shift_values.shape[0]
    per_device = shifts_all // groups
    new_count = shifts_all * COLS
    basis_count = prior_basis.shape[0]
    slab_x = prior_basis.shape[1]
    quarter = prior_basis.shape[2]
    depth = prior_basis.shape[3]
    flat_basis = prior_basis.reshape(basis_count, slab_x * quarter * depth)
    cell_weight = 1.0 / (slab_x * quarter * depth * groups * lax.axis_size("space"))
    tail_columns = prior_basis[basis_count - new_count :]
    basis_gram = allsum(products(flat_basis, flat_basis)) * cell_weight
    conduct = lookup(labels, conductance)
    capacity = lookup(labels, capacity_table)
    rimmed = padded_2(conduct, (("space", 0),), 1)
    face_list = conductances(conduct, jnp.pad(rimmed, ((0, 0), (1, 1), (1, 1))))
    shift_list = lax.dynamic_slice_in_dim(
        shift_values, lax.axis_index("shift") * per_device, per_device, 0
    )
    diagonal = diagonal_of(face_list, shift_list, capacity)
    starting = lax.all_to_all(tail_columns, "shift", split_axis=0, concat_axis=2, tiled=True)
    full_y = starting.shape[2]
    source = starting.reshape(per_device, COLS, slab_x, full_y, depth) * capacity[None, None]

    def padder(field):
        widened = padded_2(field, (("space", 2),), 1)
        return jnp.pad(widened, ((0, 0), (0, 0), (0, 0), (1, 1), (1, 1)))

    fields = chebyshev(source, face_list, diagonal, padder)
    merged = fields.reshape(per_device * COLS, slab_x, full_y, depth)
    regrouped = lax.all_to_all(merged, "shift", split_axis=2, concat_axis=0, tiled=True)
    columns = regrouped.reshape(new_count, slab_x * quarter * depth)
    sums = allsum(
        jnp.concatenate([products(columns, flat_basis), products(columns, columns)], axis=1)
    ) * cell_weight
    first_proj = sums[:, :basis_count]
    second_proj = first_proj - matmul(first_proj, basis_gram)
    coefficients = first_proj + second_proj
    columns = columns - matmul(coefficients, flat_basis)
    gram_matrix = (
        sums[:, basis_count:]
        - products(coefficients, first_proj)
        - products(first_proj, coefficients)
        + products(matmul(coefficients, basis_gram), coefficients)
    )
    factor = jnp.linalg.cholesky(gram_matrix)
    orthonormal = lax.linalg.triangular_solve(factor, columns, left_side=True, lower=True)
    new_block = orthonormal.reshape(shifts_all, COLS, slab_x, quarter, depth)
    return (new_block, coefficients, factor)


def solution(mesh):
    in_specs = (P("space", None, None), P(), P(), P(), P(None, "space", "shift", None))
    out_specs = (P(None, None, "space", "shift", None), P(), P())
    return jax.shard_map(local, mesh=mesh, in_specs=in_specs, out_specs=out_specs, check_vma=False)
```

```python
import jax
import jax.numpy as jnp
from jax import lax
from jax.sharding import PartitionSpec as P

COLS = 8
SWEEPS = 4


LOWER_BOUND = 0.1
UPPER_BOUND = 2.0


def padded_2(cells, sides, width):
    for axis, dim in sides:
        count = lax.axis_size(axis)
        ends = count - 1
        head = lax.slice_in_dim(cells, 0, width, axis=dim)
        tail = lax.slice_in_dim(cells, cells.shape[dim] - width, cells.shape[dim], axis=dim)
        cells = jnp.concatenate(
            [
                lax.ppermute(tail, axis, [(i, (i + 1) % count) for i in range(ends)]),
                cells,
                lax.ppermute(head, axis, [((i + 1) % count, i) for i in range(ends)]),
            ],
            axis=dim,
        )
    return cells


def allsum(value):
    axes = ("shift", "space")
    total = lax.axis_size("shift") * lax.axis_size("space")
    if total & (total - 1):
        return lax.psum(value, axes)
    for bit in range(total.bit_length() - 1):
        mask = 1 << bit
        value = value + lax.ppermute(value, axes, [(i, i ^ mask) for i in range(total)])
    return value


def lookup(labels, table):
    materials = jnp.arange(table.shape[0], dtype=jnp.int32)
    onehot = (labels[None] == materials[:, None, None, None]).astype(jnp.float32)
    return jnp.sum(onehot * table[:, None, None, None], axis=0)


def conductances(conduct, padded):
    west_face = 0.5 * (conduct + padded[:-2, 1:-1, 1:-1])
    east_face = 0.5 * (conduct + padded[2:, 1:-1, 1:-1])
    south_face = 0.5 * (conduct + padded[1:-1, :-2, 1:-1])
    north_face = 0.5 * (conduct + padded[1:-1, 2:, 1:-1])
    below_face = 0.5 * (conduct + padded[1:-1, 1:-1, :-2])
    above_face = 0.5 * (conduct + padded[1:-1, 1:-1, 2:])
    return (west_face, east_face, south_face, north_face, below_face, above_face)


def neighbours(padded, face_list):
    west_face, east_face, south_face, north_face, below_face, above_face = face_list
    summed = west_face * padded[..., :-2, 1:-1, 1:-1] + east_face * padded[..., 2:, 1:-1, 1:-1]
    summed = (
        summed
        + south_face * padded[..., 1:-1, :-2, 1:-1]
        + north_face * padded[..., 1:-1, 2:, 1:-1]
    )
    summed = (
        summed
        + below_face * padded[..., 1:-1, 1:-1, :-2]
        + above_face * padded[..., 1:-1, 1:-1, 2:]
    )
    return summed


def diagonal_of(face_list, shift_list, capacity):
    west_face, east_face, south_face, north_face, below_face, above_face = face_list
    summed = west_face + east_face + (south_face + north_face) + (below_face + above_face)
    return summed[None, None] + shift_list[:, None, None, None, None] * capacity[None, None]


def chebyshev(source, face_list, diagonal, padder):
    center = 0.5 * (UPPER_BOUND + LOWER_BOUND)
    spread = 0.5 * (UPPER_BOUND - LOWER_BOUND)
    ratio_value = center / spread
    reciprocal = 1.0 / diagonal
    solution = jnp.zeros_like(source)
    remainder = source
    weight_old = 1.0 / ratio_value
    direction = reciprocal * remainder / center
    for sweep_index in range(SWEEPS):
        solution = solution + direction
        if sweep_index + 1 < SWEEPS:
            applied = diagonal * direction - neighbours(padder(direction), face_list)
            remainder = remainder - applied
            weight_new = 1.0 / (2.0 * ratio_value - weight_old)
            direction = weight_new * weight_old * direction + 2.0 * weight_new / spread * (
                reciprocal * remainder
            )
            weight_old = weight_new
    return solution


def products(left_side, right_side):
    cells = tuple(range(1, left_side.ndim))
    return lax.dot_general(
        left_side, right_side, ((cells, cells), ((), ())), precision=lax.Precision.HIGHEST
    )


def expand(weights, fields):
    return lax.dot_general(
        weights, fields, (((1,), (0,)), ((), ())), precision=lax.Precision.HIGHEST
    )


def matmul(left_side, right_side):
    return jnp.dot(left_side, right_side, precision=lax.Precision.HIGHEST)


def local(labels, conductance, capacity_table, shift_values, prior_basis):
    groups = lax.axis_size("shift")
    shifts_all = shift_values.shape[0]
    per_device = shifts_all // groups
    new_count = shifts_all * COLS
    basis_count = prior_basis.shape[0]
    slab_x = prior_basis.shape[1]
    quarter = prior_basis.shape[2]
    depth = prior_basis.shape[3]
    cell_weight = 1.0 / (slab_x * quarter * depth * groups * lax.axis_size("space"))
    tail_columns = prior_basis[basis_count - new_count :]
    basis_gram = allsum(products(prior_basis, prior_basis)) * cell_weight
    conduct = lookup(labels, conductance)
    capacity = lookup(labels, capacity_table)
    rimmed = padded_2(conduct, (("space", 0),), 1)
    face_list = conductances(conduct, jnp.pad(rimmed, ((0, 0), (1, 1), (1, 1))))
    shift_list = lax.dynamic_slice_in_dim(
        shift_values, lax.axis_index("shift") * per_device, per_device, 0
    )
    diagonal = diagonal_of(face_list, shift_list, capacity)
    starting = lax.all_to_all(tail_columns, "shift", split_axis=0, concat_axis=2, tiled=True)
    full_y = starting.shape[2]
    source = starting.reshape(per_device, COLS, slab_x, full_y, depth) * capacity[None, None]

    def padder(field):
        widened = padded_2(field, (("space", 2),), 1)
        return jnp.pad(widened, ((0, 0), (0, 0), (0, 0), (1, 1), (1, 1)))

    fields = chebyshev(source, face_list, diagonal, padder)
    merged = fields.reshape(per_device * COLS, slab_x, full_y, depth)
    regrouped = lax.all_to_all(merged, "shift", split_axis=2, concat_axis=0, tiled=True)
    columns = regrouped.reshape(new_count, slab_x, quarter, depth)
    sums = allsum(
        jnp.concatenate([products(columns, prior_basis), products(columns, columns)], axis=1)
    ) * cell_weight
    first_proj = sums[:, :basis_count]
    second_proj = first_proj - matmul(first_proj, basis_gram)
    coefficients = first_proj + second_proj
    columns = columns - expand(coefficients, prior_basis)
    gram_matrix = (
        sums[:, basis_count:]
        - products(coefficients, first_proj)
        - products(first_proj, coefficients)
        + products(matmul(coefficients, basis_gram), coefficients)
    )
    factor = jnp.linalg.cholesky(gram_matrix)
    orthonormal = lax.linalg.triangular_solve(
        factor, columns.reshape(new_count, slab_x * quarter * depth), left_side=True, lower=True
    )
    new_block = orthonormal.reshape(shifts_all, COLS, slab_x, quarter, depth)
    return (new_block, coefficients, factor)


def solution(mesh):
    in_specs = (P("space", None, None), P(), P(), P(), P(None, "space", "shift", None))
    out_specs = (P(None, None, "space", "shift", None), P(), P())
    return jax.shard_map(local, mesh=mesh, in_specs=in_specs, out_specs=out_specs, check_vma=False)
```

```python
import jax
import jax.numpy as jnp
from jax import lax
from jax.sharding import PartitionSpec as P

COLS = 8
SWEEPS = 4


LOWER_BOUND = 0.1
UPPER_BOUND = 2.0


def padded_2(cells, sides, width):
    for axis, dim in sides:
        count = lax.axis_size(axis)
        ends = count - 1
        head = lax.slice_in_dim(cells, 0, width, axis=dim)
        tail = lax.slice_in_dim(cells, cells.shape[dim] - width, cells.shape[dim], axis=dim)
        cells = jnp.concatenate(
            [
                lax.ppermute(tail, axis, [(i, (i + 1) % count) for i in range(ends)]),
                cells,
                lax.ppermute(head, axis, [((i + 1) % count, i) for i in range(ends)]),
            ],
            axis=dim,
        )
    return cells


def allsum(value):
    axes = ("shift", "space")
    total = lax.axis_size("shift") * lax.axis_size("space")
    if total & (total - 1):
        return lax.psum(value, axes)
    for bit in range(total.bit_length() - 1):
        mask = 1 << bit
        value = value + lax.ppermute(value, axes, [(i, i ^ mask) for i in range(total)])
    return value


def pack_symmetric(full, half):
    row = lax.broadcasted_iota(jnp.int32, (half, half), 0)
    col = lax.broadcasted_iota(jnp.int32, (half, half), 1)
    corner = jnp.where(row > col, full[:half, :half], full[half:, half:])
    return jnp.concatenate([full[:half, half:], corner, jnp.diagonal(full[:half, :half])[None]], axis=0)


def unpack_symmetric(packed, half):
    row = lax.broadcasted_iota(jnp.int32, (half, half), 0)
    col = lax.broadcasted_iota(jnp.int32, (half, half), 1)
    upper = packed[:half]
    corner = packed[half : 2 * half]
    first = jnp.where(row > col, corner, corner.T)
    first = jnp.where(row == col, packed[2 * half][None, :], first)
    second = jnp.where(row < col, corner, corner.T)
    return jnp.concatenate(
        [jnp.concatenate([first, upper], axis=1), jnp.concatenate([upper.T, second], axis=1)], axis=0
    )


def lookup(labels, table):
    materials = jnp.arange(table.shape[0], dtype=jnp.int32)
    onehot = (labels[None] == materials[:, None, None, None]).astype(jnp.float32)
    return jnp.sum(onehot * table[:, None, None, None], axis=0)


def conductances(conduct, padded):
    west_face = 0.5 * (conduct + padded[:-2, 1:-1, 1:-1])
    east_face = 0.5 * (conduct + padded[2:, 1:-1, 1:-1])
    south_face = 0.5 * (conduct + padded[1:-1, :-2, 1:-1])
    north_face = 0.5 * (conduct + padded[1:-1, 2:, 1:-1])
    below_face = 0.5 * (conduct + padded[1:-1, 1:-1, :-2])
    above_face = 0.5 * (conduct + padded[1:-1, 1:-1, 2:])
    return (west_face, east_face, south_face, north_face, below_face, above_face)


def neighbours(padded, face_list):
    west_face, east_face, south_face, north_face, below_face, above_face = face_list
    summed = west_face * padded[..., :-2, 1:-1, 1:-1] + east_face * padded[..., 2:, 1:-1, 1:-1]
    summed = (
        summed
        + south_face * padded[..., 1:-1, :-2, 1:-1]
        + north_face * padded[..., 1:-1, 2:, 1:-1]
    )
    summed = (
        summed
        + below_face * padded[..., 1:-1, 1:-1, :-2]
        + above_face * padded[..., 1:-1, 1:-1, 2:]
    )
    return summed


def diagonal_of(face_list, shift_list, capacity):
    west_face, east_face, south_face, north_face, below_face, above_face = face_list
    summed = west_face + east_face + (south_face + north_face) + (below_face + above_face)
    return summed[None, None] + shift_list[:, None, None, None, None] * capacity[None, None]


def chebyshev(source, face_list, diagonal, padder):
    center = 0.5 * (UPPER_BOUND + LOWER_BOUND)
    spread = 0.5 * (UPPER_BOUND - LOWER_BOUND)
    ratio_value = center / spread
    reciprocal = 1.0 / diagonal
    solution = jnp.zeros_like(source)
    remainder = source
    weight_old = 1.0 / ratio_value
    direction = reciprocal * remainder / center
    for sweep_index in range(SWEEPS):
        solution = solution + direction
        if sweep_index + 1 < SWEEPS:
            applied = diagonal * direction - neighbours(padder(direction), face_list)
            remainder = remainder - applied
            weight_new = 1.0 / (2.0 * ratio_value - weight_old)
            direction = weight_new * weight_old * direction + 2.0 * weight_new / spread * (
                reciprocal * remainder
            )
            weight_old = weight_new
    return solution


def products(left_side, right_side):
    return lax.dot_general(
        left_side, right_side, (((1,), (1,)), ((), ())), precision=lax.Precision.HIGHEST
    )


def matmul(left_side, right_side):
    return jnp.dot(left_side, right_side, precision=lax.Precision.HIGHEST)


def local(labels, conductance, capacity_table, shift_values, prior_basis):
    groups = lax.axis_size("shift")
    shifts_all = shift_values.shape[0]
    per_device = shifts_all // groups
    new_count = shifts_all * COLS
    basis_count = prior_basis.shape[0]
    slab_x = prior_basis.shape[1]
    quarter = prior_basis.shape[2]
    depth = prior_basis.shape[3]
    flat_basis = prior_basis.reshape(basis_count, slab_x * quarter * depth)
    cell_weight = 1.0 / (slab_x * quarter * depth * groups * lax.axis_size("space"))
    tail_columns = prior_basis[basis_count - new_count :]
    conduct = lookup(labels, conductance)
    capacity = lookup(labels, capacity_table)
    rimmed = padded_2(conduct, (("space", 0),), 1)
    face_list = conductances(conduct, jnp.pad(rimmed, ((0, 0), (1, 1), (1, 1))))
    shift_list = lax.dynamic_slice_in_dim(
        shift_values, lax.axis_index("shift") * per_device, per_device, 0
    )
    diagonal = diagonal_of(face_list, shift_list, capacity)
    starting = lax.all_to_all(tail_columns, "shift", split_axis=0, concat_axis=2, tiled=True)
    full_y = starting.shape[2]
    source = starting.reshape(per_device, COLS, slab_x, full_y, depth) * capacity[None, None]

    def padder(field):
        widened = padded_2(field, (("space", 2),), 1)
        return jnp.pad(widened, ((0, 0), (0, 0), (0, 0), (1, 1), (1, 1)))

    fields = chebyshev(source, face_list, diagonal, padder)
    merged = fields.reshape(per_device * COLS, slab_x, full_y, depth)
    regrouped = lax.all_to_all(merged, "shift", split_axis=2, concat_axis=0, tiled=True)
    columns = regrouped.reshape(new_count, slab_x * quarter * depth)
    own = jnp.concatenate([products(columns, flat_basis), products(columns, columns)], axis=1)
    half = basis_count // 2
    packed = pack_symmetric(products(flat_basis, flat_basis), half)
    total = allsum(jnp.concatenate([own.reshape(-1, half), packed], axis=0)) * cell_weight
    sums = total[: own.size // half].reshape(own.shape)
    basis_gram = unpack_symmetric(total[own.size // half :], half)
    first_proj = sums[:, :basis_count]
    second_proj = first_proj - matmul(first_proj, basis_gram)
    coefficients = first_proj + second_proj
    columns = columns - matmul(coefficients, flat_basis)
    gram_matrix = (
        sums[:, basis_count:]
        - products(coefficients, first_proj)
        - products(first_proj, coefficients)
        + products(matmul(coefficients, basis_gram), coefficients)
    )
    factor = jnp.linalg.cholesky(gram_matrix)
    orthonormal = lax.linalg.triangular_solve(factor, columns, left_side=True, lower=True)
    new_block = orthonormal.reshape(shifts_all, COLS, slab_x, quarter, depth)
    return (new_block, coefficients, factor)


def solution(mesh):
    in_specs = (P("space", None, None), P(), P(), P(), P(None, "space", "shift", None))
    out_specs = (P(None, None, "space", "shift", None), P(), P())
    return jax.shard_map(local, mesh=mesh, in_specs=in_specs, out_specs=out_specs, check_vma=False)
```

```python
import jax
import jax.numpy as jnp
from jax import lax
from jax.sharding import PartitionSpec as P

COLS = 8
SWEEPS = 4


LOWER_BOUND = 0.1
UPPER_BOUND = 2.0


def padded_2(cells, sides, width):
    for axis, dim in sides:
        count = lax.axis_size(axis)
        ends = count - 1
        head = lax.slice_in_dim(cells, 0, width, axis=dim)
        tail = lax.slice_in_dim(cells, cells.shape[dim] - width, cells.shape[dim], axis=dim)
        cells = jnp.concatenate(
            [
                lax.ppermute(tail, axis, [(i, (i + 1) % count) for i in range(ends)]),
                cells,
                lax.ppermute(head, axis, [((i + 1) % count, i) for i in range(ends)]),
            ],
            axis=dim,
        )
    return cells


def allsum(value):
    axes = ("shift", "space")
    total = lax.axis_size("shift") * lax.axis_size("space")
    if total & (total - 1):
        return lax.psum(value, axes)
    for bit in range(total.bit_length() - 1):
        mask = 1 << bit
        value = value + lax.ppermute(value, axes, [(i, i ^ mask) for i in range(total)])
    return value


def pack_symmetric(full, half):
    row = lax.broadcasted_iota(jnp.int32, (half, half), 0)
    col = lax.broadcasted_iota(jnp.int32, (half, half), 1)
    corner = jnp.where(row > col, full[:half, :half], full[half:, half:])
    return jnp.concatenate([full[:half, half:], corner, jnp.diagonal(full[:half, :half])[None]], axis=0)


def unpack_symmetric(packed, half):
    row = lax.broadcasted_iota(jnp.int32, (half, half), 0)
    col = lax.broadcasted_iota(jnp.int32, (half, half), 1)
    upper = packed[:half]
    corner = packed[half : 2 * half]
    first = jnp.where(row > col, corner, corner.T)
    first = jnp.where(row == col, packed[2 * half][None, :], first)
    second = jnp.where(row < col, corner, corner.T)
    return jnp.concatenate(
        [jnp.concatenate([first, upper], axis=1), jnp.concatenate([upper.T, second], axis=1)], axis=0
    )


def lookup(labels, table):
    materials = jnp.arange(table.shape[0], dtype=jnp.int32)
    onehot = (labels[None] == materials[:, None, None, None]).astype(jnp.float32)
    return jnp.sum(onehot * table[:, None, None, None], axis=0)


def conductances(conduct, padded):
    west_face = 0.5 * (conduct + padded[:-2, 1:-1, 1:-1])
    east_face = 0.5 * (conduct + padded[2:, 1:-1, 1:-1])
    south_face = 0.5 * (conduct + padded[1:-1, :-2, 1:-1])
    north_face = 0.5 * (conduct + padded[1:-1, 2:, 1:-1])
    below_face = 0.5 * (conduct + padded[1:-1, 1:-1, :-2])
    above_face = 0.5 * (conduct + padded[1:-1, 1:-1, 2:])
    return (west_face, east_face, south_face, north_face, below_face, above_face)


def neighbours(padded, face_list):
    west_face, east_face, south_face, north_face, below_face, above_face = face_list
    summed = west_face * padded[..., :-2, 1:-1, 1:-1] + east_face * padded[..., 2:, 1:-1, 1:-1]
    summed = (
        summed
        + south_face * padded[..., 1:-1, :-2, 1:-1]
        + north_face * padded[..., 1:-1, 2:, 1:-1]
    )
    summed = (
        summed
        + below_face * padded[..., 1:-1, 1:-1, :-2]
        + above_face * padded[..., 1:-1, 1:-1, 2:]
    )
    return summed


def diagonal_of(face_list, shift_list, capacity):
    west_face, east_face, south_face, north_face, below_face, above_face = face_list
    summed = west_face + east_face + (south_face + north_face) + (below_face + above_face)
    return summed[None, None] + shift_list[:, None, None, None, None] * capacity[None, None]


def chebyshev(source, face_list, diagonal, padder, anchor):
    center = 0.5 * (UPPER_BOUND + LOWER_BOUND)
    spread = 0.5 * (UPPER_BOUND - LOWER_BOUND)
    ratio_value = center / spread
    reciprocal = 1.0 / diagonal
    solution = jnp.zeros_like(source)
    remainder = source
    weight_old = 1.0 / ratio_value
    direction = reciprocal * remainder / center
    for sweep_index in range(SWEEPS):
        solution = solution + direction
        if sweep_index + 1 < SWEEPS:
            padded = padder(direction)
            if sweep_index == 0:
                anchor, padded = lax.optimization_barrier((anchor, padded))
            applied = diagonal * direction - neighbours(padded, face_list)
            remainder = remainder - applied
            weight_new = 1.0 / (2.0 * ratio_value - weight_old)
            direction = weight_new * weight_old * direction + 2.0 * weight_new / spread * (
                reciprocal * remainder
            )
            weight_old = weight_new
    return solution, anchor


def products(left_side, right_side):
    return lax.dot_general(
        left_side, right_side, (((1,), (1,)), ((), ())), precision=lax.Precision.HIGHEST
    )


def matmul(left_side, right_side):
    return jnp.dot(left_side, right_side, precision=lax.Precision.HIGHEST)


def local(labels, conductance, capacity_table, shift_values, prior_basis):
    groups = lax.axis_size("shift")
    shifts_all = shift_values.shape[0]
    per_device = shifts_all // groups
    new_count = shifts_all * COLS
    basis_count = prior_basis.shape[0]
    slab_x = prior_basis.shape[1]
    quarter = prior_basis.shape[2]
    depth = prior_basis.shape[3]
    flat_basis = prior_basis.reshape(basis_count, slab_x * quarter * depth)
    cell_weight = 1.0 / (slab_x * quarter * depth * groups * lax.axis_size("space"))
    tail_columns = prior_basis[basis_count - new_count :]
    conduct = lookup(labels, conductance)
    capacity = lookup(labels, capacity_table)
    rimmed = padded_2(conduct, (("space", 0),), 1)
    face_list = conductances(conduct, jnp.pad(rimmed, ((0, 0), (1, 1), (1, 1))))
    shift_list = lax.dynamic_slice_in_dim(
        shift_values, lax.axis_index("shift") * per_device, per_device, 0
    )
    diagonal = diagonal_of(face_list, shift_list, capacity)
    starting = lax.all_to_all(tail_columns, "shift", split_axis=0, concat_axis=2, tiled=True)
    full_y = starting.shape[2]
    source = starting.reshape(per_device, COLS, slab_x, full_y, depth) * capacity[None, None]

    def padder(field):
        widened = padded_2(field, (("space", 2),), 1)
        return jnp.pad(widened, ((0, 0), (0, 0), (0, 0), (1, 1), (1, 1)))

    half = basis_count // 2
    packed = pack_symmetric(products(flat_basis, flat_basis), half)
    fields, packed = chebyshev(source, face_list, diagonal, padder, packed)
    merged = fields.reshape(per_device * COLS, slab_x, full_y, depth)
    regrouped = lax.all_to_all(merged, "shift", split_axis=2, concat_axis=0, tiled=True)
    columns = regrouped.reshape(new_count, slab_x * quarter * depth)
    own = jnp.concatenate([products(columns, flat_basis), products(columns, columns)], axis=1)
    total = allsum(jnp.concatenate([own.reshape(-1, half), packed], axis=0)) * cell_weight
    sums = total[: own.size // half].reshape(own.shape)
    basis_gram = unpack_symmetric(total[own.size // half :], half)
    first_proj = sums[:, :basis_count]
    second_proj = first_proj - matmul(first_proj, basis_gram)
    coefficients = first_proj + second_proj
    columns = columns - matmul(coefficients, flat_basis)
    gram_matrix = (
        sums[:, basis_count:]
        - products(coefficients, first_proj)
        - products(first_proj, coefficients)
        + products(matmul(coefficients, basis_gram), coefficients)
    )
    factor = jnp.linalg.cholesky(gram_matrix)
    orthonormal = lax.linalg.triangular_solve(factor, columns, left_side=True, lower=True)
    new_block = orthonormal.reshape(shifts_all, COLS, slab_x, quarter, depth)
    return (new_block, coefficients, factor)


def solution(mesh):
    in_specs = (P("space", None, None), P(), P(), P(), P(None, "space", "shift", None))
    out_specs = (P(None, None, "space", "shift", None), P(), P())
    return jax.shard_map(local, mesh=mesh, in_specs=in_specs, out_specs=out_specs, check_vma=False)
```

```python
import jax
import jax.numpy as jnp
from jax import lax
from jax.sharding import PartitionSpec as P

COLS = 8
SWEEPS = 4


LOWER_BOUND = 0.1
UPPER_BOUND = 2.0


def padded_2(cells, sides, width):
    for axis, dim in sides:
        count = lax.axis_size(axis)
        ends = count - 1
        head = lax.slice_in_dim(cells, 0, width, axis=dim)
        tail = lax.slice_in_dim(cells, cells.shape[dim] - width, cells.shape[dim], axis=dim)
        cells = jnp.concatenate(
            [
                lax.ppermute(tail, axis, [(i, (i + 1) % count) for i in range(ends)]),
                cells,
                lax.ppermute(head, axis, [((i + 1) % count, i) for i in range(ends)]),
            ],
            axis=dim,
        )
    return cells


def allsum(value):
    axes = ("shift", "space")
    total = lax.axis_size("shift") * lax.axis_size("space")
    if total & (total - 1):
        return lax.psum(value, axes)
    for bit in range(total.bit_length() - 1):
        mask = 1 << bit
        value = value + lax.ppermute(value, axes, [(i, i ^ mask) for i in range(total)])
    return value


def pack_symmetric(full, half):
    row = lax.broadcasted_iota(jnp.int32, (half, half), 0)
    col = lax.broadcasted_iota(jnp.int32, (half, half), 1)
    corner = jnp.where(row > col, full[:half, :half], full[half:, half:])
    return jnp.concatenate([full[:half, half:], corner, jnp.diagonal(full[:half, :half])[None]], axis=0)


def unpack_symmetric(packed, half):
    row = lax.broadcasted_iota(jnp.int32, (half, half), 0)
    col = lax.broadcasted_iota(jnp.int32, (half, half), 1)
    upper = packed[:half]
    corner = packed[half : 2 * half]
    first = jnp.where(row > col, corner, corner.T)
    first = jnp.where(row == col, packed[2 * half][None, :], first)
    second = jnp.where(row < col, corner, corner.T)
    return jnp.concatenate(
        [jnp.concatenate([first, upper], axis=1), jnp.concatenate([upper.T, second], axis=1)], axis=0
    )


def lookup(labels, table):
    materials = jnp.arange(table.shape[0], dtype=jnp.int32)
    onehot = (labels[None] == materials[:, None, None, None]).astype(jnp.float32)
    return jnp.sum(onehot * table[:, None, None, None], axis=0)


def conductances(conduct, padded):
    west_face = 0.5 * (conduct + padded[:-2, 1:-1, 1:-1])
    east_face = 0.5 * (conduct + padded[2:, 1:-1, 1:-1])
    south_face = 0.5 * (conduct + padded[1:-1, :-2, 1:-1])
    north_face = 0.5 * (conduct + padded[1:-1, 2:, 1:-1])
    below_face = 0.5 * (conduct + padded[1:-1, 1:-1, :-2])
    above_face = 0.5 * (conduct + padded[1:-1, 1:-1, 2:])
    return (west_face, east_face, south_face, north_face, below_face, above_face)


def neighbours(padded, face_list):
    west_face, east_face, south_face, north_face, below_face, above_face = face_list
    summed = west_face * padded[..., :-2, 1:-1, 1:-1] + east_face * padded[..., 2:, 1:-1, 1:-1]
    summed = (
        summed
        + south_face * padded[..., 1:-1, :-2, 1:-1]
        + north_face * padded[..., 1:-1, 2:, 1:-1]
    )
    summed = (
        summed
        + below_face * padded[..., 1:-1, 1:-1, :-2]
        + above_face * padded[..., 1:-1, 1:-1, 2:]
    )
    return summed


def diagonal_of(face_list, shift_list, capacity):
    west_face, east_face, south_face, north_face, below_face, above_face = face_list
    summed = west_face + east_face + (south_face + north_face) + (below_face + above_face)
    return summed[None, None] + shift_list[:, None, None, None, None] * capacity[None, None]


def chebyshev(source, face_list, diagonal, padder, tie, anchor_of):
    center = 0.5 * (UPPER_BOUND + LOWER_BOUND)
    spread = 0.5 * (UPPER_BOUND - LOWER_BOUND)
    ratio_value = center / spread
    reciprocal = 1.0 / diagonal
    solution = jnp.zeros_like(source)
    remainder = source
    weight_old = 1.0 / ratio_value
    direction = reciprocal * remainder / center
    for sweep_index in range(SWEEPS):
        solution = solution + direction
        if sweep_index + 1 < SWEEPS:
            if sweep_index == 0:
                tie, direction = lax.optimization_barrier((tie, direction))
            padded = padder(direction)
            if sweep_index == 0:
                anchor, padded = lax.optimization_barrier((anchor_of(tie), padded))
            applied = diagonal * direction - neighbours(padded, face_list)
            remainder = remainder - applied
            weight_new = 1.0 / (2.0 * ratio_value - weight_old)
            direction = weight_new * weight_old * direction + 2.0 * weight_new / spread * (
                reciprocal * remainder
            )
            weight_old = weight_new
    return solution, anchor


def products(left_side, right_side):
    return lax.dot_general(
        left_side, right_side, (((1,), (1,)), ((), ())), precision=lax.Precision.HIGHEST
    )


def matmul(left_side, right_side):
    return jnp.dot(left_side, right_side, precision=lax.Precision.HIGHEST)


def local(labels, conductance, capacity_table, shift_values, prior_basis):
    groups = lax.axis_size("shift")
    shifts_all = shift_values.shape[0]
    per_device = shifts_all // groups
    new_count = shifts_all * COLS
    basis_count = prior_basis.shape[0]
    slab_x = prior_basis.shape[1]
    quarter = prior_basis.shape[2]
    depth = prior_basis.shape[3]
    flat_basis = prior_basis.reshape(basis_count, slab_x * quarter * depth)
    cell_weight = 1.0 / (slab_x * quarter * depth * groups * lax.axis_size("space"))
    tail_columns = prior_basis[basis_count - new_count :]
    conduct = lookup(labels, conductance)
    capacity = lookup(labels, capacity_table)
    rimmed = padded_2(conduct, (("space", 0),), 1)
    face_list = conductances(conduct, jnp.pad(rimmed, ((0, 0), (1, 1), (1, 1))))
    shift_list = lax.dynamic_slice_in_dim(
        shift_values, lax.axis_index("shift") * per_device, per_device, 0
    )
    diagonal = diagonal_of(face_list, shift_list, capacity)
    starting = lax.all_to_all(tail_columns, "shift", split_axis=0, concat_axis=2, tiled=True)
    full_y = starting.shape[2]
    source = starting.reshape(per_device, COLS, slab_x, full_y, depth) * capacity[None, None]

    def padder(field):
        widened = padded_2(field, (("space", 2),), 1)
        return jnp.pad(widened, ((0, 0), (0, 0), (0, 0), (1, 1), (1, 1)))

    half = basis_count // 2

    def gram_of(basis):
        return pack_symmetric(products(basis, basis), half)

    fields, packed = chebyshev(source, face_list, diagonal, padder, flat_basis, gram_of)
    merged = fields.reshape(per_device * COLS, slab_x, full_y, depth)
    regrouped = lax.all_to_all(merged, "shift", split_axis=2, concat_axis=0, tiled=True)
    columns = regrouped.reshape(new_count, slab_x * quarter * depth)
    own = jnp.concatenate([products(columns, flat_basis), products(columns, columns)], axis=1)
    total = allsum(jnp.concatenate([own.reshape(-1, half), packed], axis=0)) * cell_weight
    sums = total[: own.size // half].reshape(own.shape)
    basis_gram = unpack_symmetric(total[own.size // half :], half)
    first_proj = sums[:, :basis_count]
    second_proj = first_proj - matmul(first_proj, basis_gram)
    coefficients = first_proj + second_proj
    columns = columns - matmul(coefficients, flat_basis)
    gram_matrix = (
        sums[:, basis_count:]
        - products(coefficients, first_proj)
        - products(first_proj, coefficients)
        + products(matmul(coefficients, basis_gram), coefficients)
    )
    factor = jnp.linalg.cholesky(gram_matrix)
    orthonormal = lax.linalg.triangular_solve(factor, columns, left_side=True, lower=True)
    new_block = orthonormal.reshape(shifts_all, COLS, slab_x, quarter, depth)
    return (new_block, coefficients, factor)


def solution(mesh):
    in_specs = (P("space", None, None), P(), P(), P(), P(None, "space", "shift", None))
    out_specs = (P(None, None, "space", "shift", None), P(), P())
    return jax.shard_map(local, mesh=mesh, in_specs=in_specs, out_specs=out_specs, check_vma=False)
```

```python
import jax
import jax.numpy as jnp
from jax import lax
from jax.sharding import PartitionSpec as P

COLS = 8
SWEEPS = 4


LOWER_BOUND = 0.1
UPPER_BOUND = 2.0


def padded_2(cells, sides, width):
    for axis, dim in sides:
        count = lax.axis_size(axis)
        ends = count - 1
        head = lax.slice_in_dim(cells, 0, width, axis=dim)
        tail = lax.slice_in_dim(cells, cells.shape[dim] - width, cells.shape[dim], axis=dim)
        cells = jnp.concatenate(
            [
                lax.ppermute(tail, axis, [(i, (i + 1) % count) for i in range(ends)]),
                cells,
                lax.ppermute(head, axis, [((i + 1) % count, i) for i in range(ends)]),
            ],
            axis=dim,
        )
    return cells


def exchange(value, axes, total, mask):
    return lax.ppermute(value, axes, [(i, i ^ mask) for i in range(total)])


def allsum(value, split_bits=()):
    axes = ("shift", "space")
    total = lax.axis_size("shift") * lax.axis_size("space")
    if total & (total - 1):
        return lax.psum(value, axes)
    bits = [bit for bit in range(total.bit_length() - 1) if bit not in split_bits]
    split_bits = [bit for bit in split_bits if (1 << bit) < total]
    rows = value.shape[0]
    parts = 1 << len(split_bits)
    padded_rows = -(-rows // parts) * parts
    value = jnp.pad(value, ((0, padded_rows - rows),) + ((0, 0),) * (value.ndim - 1))
    me = lax.axis_index("shift") * lax.axis_size("space") + lax.axis_index("space")
    for bit in split_bits:
        side = (me >> bit) & 1
        halves = value.reshape((2, value.shape[0] // 2) + value.shape[1:])
        keep = lax.dynamic_index_in_dim(halves, side, 0, keepdims=False)
        give = lax.dynamic_index_in_dim(halves, 1 - side, 0, keepdims=False)
        value = keep + exchange(give, axes, total, 1 << bit)
    for bit in bits:
        value = value + exchange(value, axes, total, 1 << bit)
    for bit in reversed(split_bits):
        side = (me >> bit) & 1
        other = exchange(value, axes, total, 1 << bit)
        value = jnp.where(
            side == 0,
            jnp.concatenate([value, other], axis=0),
            jnp.concatenate([other, value], axis=0),
        )
    return value[:rows]


def pack_symmetric(full, half):
    row = lax.broadcasted_iota(jnp.int32, (half, half), 0)
    col = lax.broadcasted_iota(jnp.int32, (half, half), 1)
    corner = jnp.where(row > col, full[:half, :half], full[half:, half:])
    return jnp.concatenate([full[:half, half:], corner, jnp.diagonal(full[:half, :half])[None]], axis=0)


def unpack_symmetric(packed, half):
    row = lax.broadcasted_iota(jnp.int32, (half, half), 0)
    col = lax.broadcasted_iota(jnp.int32, (half, half), 1)
    upper = packed[:half]
    corner = packed[half : 2 * half]
    first = jnp.where(row > col, corner, corner.T)
    first = jnp.where(row == col, packed[2 * half][None, :], first)
    second = jnp.where(row < col, corner, corner.T)
    return jnp.concatenate(
        [jnp.concatenate([first, upper], axis=1), jnp.concatenate([upper.T, second], axis=1)], axis=0
    )


def lookup(labels, table):
    materials = jnp.arange(table.shape[0], dtype=jnp.int32)
    onehot = (labels[None] == materials[:, None, None, None]).astype(jnp.float32)
    return jnp.sum(onehot * table[:, None, None, None], axis=0)


def conductances(conduct, padded):
    west_face = 0.5 * (conduct + padded[:-2, 1:-1, 1:-1])
    east_face = 0.5 * (conduct + padded[2:, 1:-1, 1:-1])
    south_face = 0.5 * (conduct + padded[1:-1, :-2, 1:-1])
    north_face = 0.5 * (conduct + padded[1:-1, 2:, 1:-1])
    below_face = 0.5 * (conduct + padded[1:-1, 1:-1, :-2])
    above_face = 0.5 * (conduct + padded[1:-1, 1:-1, 2:])
    return (west_face, east_face, south_face, north_face, below_face, above_face)


def neighbours(padded, face_list):
    west_face, east_face, south_face, north_face, below_face, above_face = face_list
    summed = west_face * padded[..., :-2, 1:-1, 1:-1] + east_face * padded[..., 2:, 1:-1, 1:-1]
    summed = (
        summed
        + south_face * padded[..., 1:-1, :-2, 1:-1]
        + north_face * padded[..., 1:-1, 2:, 1:-1]
    )
    summed = (
        summed
        + below_face * padded[..., 1:-1, 1:-1, :-2]
        + above_face * padded[..., 1:-1, 1:-1, 2:]
    )
    return summed


def diagonal_of(face_list, shift_list, capacity):
    west_face, east_face, south_face, north_face, below_face, above_face = face_list
    summed = west_face + east_face + (south_face + north_face) + (below_face + above_face)
    return summed[None, None] + shift_list[:, None, None, None, None] * capacity[None, None]


def chebyshev(source, face_list, diagonal, padder, tie, anchor_of):
    center = 0.5 * (UPPER_BOUND + LOWER_BOUND)
    spread = 0.5 * (UPPER_BOUND - LOWER_BOUND)
    ratio_value = center / spread
    reciprocal = 1.0 / diagonal
    solution = jnp.zeros_like(source)
    remainder = source
    weight_old = 1.0 / ratio_value
    direction = reciprocal * remainder / center
    for sweep_index in range(SWEEPS):
        solution = solution + direction
        if sweep_index + 1 < SWEEPS:
            if sweep_index == 0:
                tie, direction = lax.optimization_barrier((tie, direction))
            padded = padder(direction)
            if sweep_index == 0:
                anchor, padded = lax.optimization_barrier((anchor_of(tie), padded))
            applied = diagonal * direction - neighbours(padded, face_list)
            remainder = remainder - applied
            weight_new = 1.0 / (2.0 * ratio_value - weight_old)
            direction = weight_new * weight_old * direction + 2.0 * weight_new / spread * (
                reciprocal * remainder
            )
            weight_old = weight_new
    return solution, anchor


def products(left_side, right_side):
    return lax.dot_general(
        left_side, right_side, (((1,), (1,)), ((), ())), precision=lax.Precision.HIGHEST
    )


def matmul(left_side, right_side):
    return jnp.dot(left_side, right_side, precision=lax.Precision.HIGHEST)


def local(labels, conductance, capacity_table, shift_values, prior_basis):
    groups = lax.axis_size("shift")
    shifts_all = shift_values.shape[0]
    per_device = shifts_all // groups
    new_count = shifts_all * COLS
    basis_count = prior_basis.shape[0]
    slab_x = prior_basis.shape[1]
    quarter = prior_basis.shape[2]
    depth = prior_basis.shape[3]
    flat_basis = prior_basis.reshape(basis_count, slab_x * quarter * depth)
    cell_weight = 1.0 / (slab_x * quarter * depth * groups * lax.axis_size("space"))
    tail_columns = prior_basis[basis_count - new_count :]
    conduct = lookup(labels, conductance)
    capacity = lookup(labels, capacity_table)
    rimmed = padded_2(conduct, (("space", 0),), 1)
    face_list = conductances(conduct, jnp.pad(rimmed, ((0, 0), (1, 1), (1, 1))))
    shift_list = lax.dynamic_slice_in_dim(
        shift_values, lax.axis_index("shift") * per_device, per_device, 0
    )
    diagonal = diagonal_of(face_list, shift_list, capacity)
    starting = lax.all_to_all(tail_columns, "shift", split_axis=0, concat_axis=2, tiled=True)
    full_y = starting.shape[2]
    source = starting.reshape(per_device, COLS, slab_x, full_y, depth) * capacity[None, None]

    def padder(field):
        widened = padded_2(field, (("space", 2),), 1)
        return jnp.pad(widened, ((0, 0), (0, 0), (0, 0), (1, 1), (1, 1)))

    half = basis_count // 2

    def gram_of(basis):
        return pack_symmetric(products(basis, basis), half)

    fields, packed = chebyshev(source, face_list, diagonal, padder, flat_basis, gram_of)
    merged = fields.reshape(per_device * COLS, slab_x, full_y, depth)
    regrouped = lax.all_to_all(merged, "shift", split_axis=2, concat_axis=0, tiled=True)
    columns = regrouped.reshape(new_count, slab_x * quarter * depth)
    own = jnp.concatenate([products(columns, flat_basis), products(columns, columns)], axis=1)
    total = allsum(jnp.concatenate([own.reshape(-1, half), packed], axis=0), (3, 6)) * cell_weight
    sums = total[: own.size // half].reshape(own.shape)
    basis_gram = unpack_symmetric(total[own.size // half :], half)
    first_proj = sums[:, :basis_count]
    second_proj = first_proj - matmul(first_proj, basis_gram)
    coefficients = first_proj + second_proj
    columns = columns - matmul(coefficients, flat_basis)
    gram_matrix = (
        sums[:, basis_count:]
        - products(coefficients, first_proj)
        - products(first_proj, coefficients)
        + products(matmul(coefficients, basis_gram), coefficients)
    )
    factor = jnp.linalg.cholesky(gram_matrix)
    orthonormal = lax.linalg.triangular_solve(factor, columns, left_side=True, lower=True)
    new_block = orthonormal.reshape(shifts_all, COLS, slab_x, quarter, depth)
    return (new_block, coefficients, factor)


def solution(mesh):
    in_specs = (P("space", None, None), P(), P(), P(), P(None, "space", "shift", None))
    out_specs = (P(None, None, "space", "shift", None), P(), P())
    return jax.shard_map(local, mesh=mesh, in_specs=in_specs, out_specs=out_specs, check_vma=False)
```

```python
import jax
import jax.numpy as jnp
from jax import lax
from jax.sharding import PartitionSpec as P

COLS = 8
SWEEPS = 4


LOWER_BOUND = 0.1
UPPER_BOUND = 2.0


def padded_2(cells, sides, width):
    for axis, dim in sides:
        count = lax.axis_size(axis)
        ends = count - 1
        head = lax.slice_in_dim(cells, 0, width, axis=dim)
        tail = lax.slice_in_dim(cells, cells.shape[dim] - width, cells.shape[dim], axis=dim)
        cells = jnp.concatenate(
            [
                lax.ppermute(tail, axis, [(i, (i + 1) % count) for i in range(ends)]),
                cells,
                lax.ppermute(head, axis, [((i + 1) % count, i) for i in range(ends)]),
            ],
            axis=dim,
        )
    return cells


def exchange(value, axes, total, mask):
    return lax.ppermute(value, axes, [(i, i ^ mask) for i in range(total)])


def allsum(value, split_bits=()):
    axes = ("shift", "space")
    total = lax.axis_size("shift") * lax.axis_size("space")
    if total & (total - 1):
        return lax.psum(value, axes)
    bits = [bit for bit in range(total.bit_length() - 1) if bit not in split_bits]
    split_bits = [bit for bit in split_bits if (1 << bit) < total]
    rows = value.shape[0]
    parts = 1 << len(split_bits)
    padded_rows = -(-rows // parts) * parts
    value = jnp.pad(value, ((0, padded_rows - rows),) + ((0, 0),) * (value.ndim - 1))
    me = lax.axis_index("shift") * lax.axis_size("space") + lax.axis_index("space")
    for bit in split_bits:
        side = (me >> bit) & 1
        halves = value.reshape((2, value.shape[0] // 2) + value.shape[1:])
        keep = lax.dynamic_index_in_dim(halves, side, 0, keepdims=False)
        give = lax.dynamic_index_in_dim(halves, 1 - side, 0, keepdims=False)
        value = keep + exchange(give, axes, total, 1 << bit)
    for bit in bits:
        value = value + exchange(value, axes, total, 1 << bit)
    for bit in reversed(split_bits):
        side = (me >> bit) & 1
        other = exchange(value, axes, total, 1 << bit)
        value = jnp.where(
            side == 0,
            jnp.concatenate([value, other], axis=0),
            jnp.concatenate([other, value], axis=0),
        )
    return value[:rows]


def pack_symmetric(full, half):
    row = lax.broadcasted_iota(jnp.int32, (half, half), 0)
    col = lax.broadcasted_iota(jnp.int32, (half, half), 1)
    corner = jnp.where(row > col, full[:half, :half], full[half:, half:])
    return jnp.concatenate([full[:half, half:], corner, jnp.diagonal(full[:half, :half])[None]], axis=0)


def unpack_symmetric(packed, half):
    row = lax.broadcasted_iota(jnp.int32, (half, half), 0)
    col = lax.broadcasted_iota(jnp.int32, (half, half), 1)
    upper = packed[:half]
    corner = packed[half : 2 * half]
    first = jnp.where(row > col, corner, corner.T)
    first = jnp.where(row == col, packed[2 * half][None, :], first)
    second = jnp.where(row < col, corner, corner.T)
    return jnp.concatenate(
        [jnp.concatenate([first, upper], axis=1), jnp.concatenate([upper.T, second], axis=1)], axis=0
    )


def lookup(labels, table):
    materials = jnp.arange(table.shape[0], dtype=jnp.int32)
    onehot = (labels[None] == materials[:, None, None, None]).astype(jnp.float32)
    return jnp.sum(onehot * table[:, None, None, None], axis=0)


def conductances(conduct, padded):
    west_face = 0.5 * (conduct + padded[:-2, 1:-1, 1:-1])
    east_face = 0.5 * (conduct + padded[2:, 1:-1, 1:-1])
    south_face = 0.5 * (conduct + padded[1:-1, :-2, 1:-1])
    north_face = 0.5 * (conduct + padded[1:-1, 2:, 1:-1])
    below_face = 0.5 * (conduct + padded[1:-1, 1:-1, :-2])
    above_face = 0.5 * (conduct + padded[1:-1, 1:-1, 2:])
    return (west_face, east_face, south_face, north_face, below_face, above_face)


def neighbours(padded, face_list):
    west_face, east_face, south_face, north_face, below_face, above_face = face_list
    summed = west_face * padded[..., :-2, 1:-1, 1:-1] + east_face * padded[..., 2:, 1:-1, 1:-1]
    summed = (
        summed
        + south_face * padded[..., 1:-1, :-2, 1:-1]
        + north_face * padded[..., 1:-1, 2:, 1:-1]
    )
    summed = (
        summed
        + below_face * padded[..., 1:-1, 1:-1, :-2]
        + above_face * padded[..., 1:-1, 1:-1, 2:]
    )
    return summed


def diagonal_of(face_list, shift_list, capacity):
    west_face, east_face, south_face, north_face, below_face, above_face = face_list
    summed = west_face + east_face + (south_face + north_face) + (below_face + above_face)
    return summed[None, None] + shift_list[:, None, None, None, None] * capacity[None, None]


def chebyshev(source, face_list, diagonal, padder, tie, anchor_of):
    center = 0.5 * (UPPER_BOUND + LOWER_BOUND)
    spread = 0.5 * (UPPER_BOUND - LOWER_BOUND)
    ratio_value = center / spread
    reciprocal = 1.0 / diagonal
    solution = jnp.zeros_like(source)
    remainder = source
    weight_old = 1.0 / ratio_value
    direction = reciprocal * remainder / center
    for sweep_index in range(SWEEPS):
        solution = solution + direction
        if sweep_index + 1 < SWEEPS:
            if sweep_index == 0:
                tie, direction = lax.optimization_barrier((tie, direction))
            padded = padder(direction)
            if sweep_index == 0:
                anchor, padded = lax.optimization_barrier((anchor_of(tie), padded))
            applied = diagonal * direction - neighbours(padded, face_list)
            remainder = remainder - applied
            weight_new = 1.0 / (2.0 * ratio_value - weight_old)
            direction = weight_new * weight_old * direction + 2.0 * weight_new / spread * (
                reciprocal * remainder
            )
            weight_old = weight_new
    return solution, anchor


def products(left_side, right_side):
    return lax.dot_general(
        left_side, right_side, (((1,), (1,)), ((), ())), precision=lax.Precision.HIGHEST
    )


def matmul(left_side, right_side):
    return jnp.dot(left_side, right_side, precision=lax.Precision.HIGHEST)


def local(labels, conductance, capacity_table, shift_values, prior_basis):
    groups = lax.axis_size("shift")
    shifts_all = shift_values.shape[0]
    per_device = shifts_all // groups
    new_count = shifts_all * COLS
    basis_count = prior_basis.shape[0]
    slab_x = prior_basis.shape[1]
    quarter = prior_basis.shape[2]
    depth = prior_basis.shape[3]
    flat_basis = prior_basis.reshape(basis_count, slab_x * quarter * depth)
    cell_weight = 1.0 / (slab_x * quarter * depth * groups * lax.axis_size("space"))
    tail_columns = prior_basis[basis_count - new_count :]
    conduct = lookup(labels, conductance)
    capacity = lookup(labels, capacity_table)
    rimmed = padded_2(conduct, (("space", 0),), 1)
    face_list = conductances(conduct, jnp.pad(rimmed, ((0, 0), (1, 1), (1, 1))))
    shift_list = lax.dynamic_slice_in_dim(
        shift_values, lax.axis_index("shift") * per_device, per_device, 0
    )
    diagonal = diagonal_of(face_list, shift_list, capacity)
    starting = lax.all_to_all(tail_columns, "shift", split_axis=0, concat_axis=2, tiled=True)
    full_y = starting.shape[2]
    source = starting.reshape(per_device, COLS, slab_x, full_y, depth) * capacity[None, None]

    def padder(field):
        widened = padded_2(field, (("space", 2),), 1)
        return jnp.pad(widened, ((0, 0), (0, 0), (0, 0), (1, 1), (1, 1)))

    half = basis_count // 2

    def gram_of(basis):
        return pack_symmetric(products(basis, basis), half)

    fields, packed = chebyshev(source, face_list, diagonal, padder, flat_basis, gram_of)
    merged = fields.reshape(per_device * COLS, slab_x, full_y, depth)
    regrouped = lax.all_to_all(merged, "shift", split_axis=2, concat_axis=0, tiled=True)
    columns = regrouped.reshape(new_count, slab_x * quarter * depth)
    own = jnp.concatenate([products(columns, flat_basis), products(columns, columns)], axis=1)
    total = allsum(jnp.concatenate([own.reshape(-1, half), packed], axis=0), (3, 6)) * cell_weight
    sums = total[: own.size // half].reshape(own.shape)
    basis_gram = unpack_symmetric(total[own.size // half :], half)
    first_proj = sums[:, :basis_count]
    second_proj = first_proj - matmul(first_proj, basis_gram)
    coefficients = first_proj + second_proj
    gram_matrix = (
        sums[:, basis_count:]
        - products(coefficients, first_proj)
        - products(first_proj, coefficients)
        + products(matmul(coefficients, basis_gram), coefficients)
    )
    factor = jnp.linalg.cholesky(gram_matrix)
    inverse = lax.linalg.triangular_solve(
        factor, jnp.eye(new_count, dtype=factor.dtype), left_side=True, lower=True
    )
    orthonormal = matmul(inverse, columns) - matmul(matmul(inverse, coefficients), flat_basis)
    new_block = orthonormal.reshape(shifts_all, COLS, slab_x, quarter, depth)
    return (new_block, coefficients, factor)


def solution(mesh):
    in_specs = (P("space", None, None), P(), P(), P(), P(None, "space", "shift", None))
    out_specs = (P(None, None, "space", "shift", None), P(), P())
    return jax.shard_map(local, mesh=mesh, in_specs=in_specs, out_specs=out_specs, check_vma=False)
```

```python
import jax
import jax.numpy as jnp
from jax import lax
from jax.sharding import PartitionSpec as P

COLS = 8
SWEEPS = 4


LOWER_BOUND = 0.1
UPPER_BOUND = 2.0


def padded_2(cells, sides, width):
    for axis, dim in sides:
        count = lax.axis_size(axis)
        ends = count - 1
        head = lax.slice_in_dim(cells, 0, width, axis=dim)
        tail = lax.slice_in_dim(cells, cells.shape[dim] - width, cells.shape[dim], axis=dim)
        cells = jnp.concatenate(
            [
                lax.ppermute(tail, axis, [(i, (i + 1) % count) for i in range(ends)]),
                cells,
                lax.ppermute(head, axis, [((i + 1) % count, i) for i in range(ends)]),
            ],
            axis=dim,
        )
    return cells


def exchange(value, axes, total, mask):
    return lax.ppermute(value, axes, [(i, i ^ mask) for i in range(total)])


def allsum(value, split_bits=()):
    axes = ("shift", "space")
    total = lax.axis_size("shift") * lax.axis_size("space")
    if total & (total - 1):
        return lax.psum(value, axes)
    bits = [bit for bit in range(total.bit_length() - 1) if bit not in split_bits]
    split_bits = [bit for bit in split_bits if (1 << bit) < total]
    rows = value.shape[0]
    parts = 1 << len(split_bits)
    padded_rows = -(-rows // parts) * parts
    value = jnp.pad(value, ((0, padded_rows - rows),) + ((0, 0),) * (value.ndim - 1))
    me = lax.axis_index("shift") * lax.axis_size("space") + lax.axis_index("space")
    for bit in split_bits:
        side = (me >> bit) & 1
        halves = value.reshape((2, value.shape[0] // 2) + value.shape[1:])
        keep = lax.dynamic_index_in_dim(halves, side, 0, keepdims=False)
        give = lax.dynamic_index_in_dim(halves, 1 - side, 0, keepdims=False)
        value = keep + exchange(give, axes, total, 1 << bit)
    for bit in bits:
        value = value + exchange(value, axes, total, 1 << bit)
    for bit in reversed(split_bits):
        side = (me >> bit) & 1
        other = exchange(value, axes, total, 1 << bit)
        value = jnp.where(
            side == 0,
            jnp.concatenate([value, other], axis=0),
            jnp.concatenate([other, value], axis=0),
        )
    return value[:rows]


def pack_symmetric(full, half):
    row = lax.broadcasted_iota(jnp.int32, (half, half), 0)
    col = lax.broadcasted_iota(jnp.int32, (half, half), 1)
    corner = jnp.where(row > col, full[:half, :half], full[half:, half:])
    return jnp.concatenate([full[:half, half:], corner, jnp.diagonal(full[:half, :half])[None]], axis=0)


def unpack_symmetric(packed, half):
    row = lax.broadcasted_iota(jnp.int32, (half, half), 0)
    col = lax.broadcasted_iota(jnp.int32, (half, half), 1)
    upper = packed[:half]
    corner = packed[half : 2 * half]
    first = jnp.where(row > col, corner, corner.T)
    first = jnp.where(row == col, packed[2 * half][None, :], first)
    second = jnp.where(row < col, corner, corner.T)
    return jnp.concatenate(
        [jnp.concatenate([first, upper], axis=1), jnp.concatenate([upper.T, second], axis=1)], axis=0
    )


def lookup(labels, table):
    materials = jnp.arange(table.shape[0], dtype=jnp.int32)
    onehot = (labels[None] == materials[:, None, None, None]).astype(jnp.float32)
    return jnp.sum(onehot * table[:, None, None, None], axis=0)


def conductances(conduct, padded):
    west_face = 0.5 * (conduct + padded[:-2, 1:-1, 1:-1])
    east_face = 0.5 * (conduct + padded[2:, 1:-1, 1:-1])
    south_face = 0.5 * (conduct + padded[1:-1, :-2, 1:-1])
    north_face = 0.5 * (conduct + padded[1:-1, 2:, 1:-1])
    below_face = 0.5 * (conduct + padded[1:-1, 1:-1, :-2])
    above_face = 0.5 * (conduct + padded[1:-1, 1:-1, 2:])
    return (west_face, east_face, south_face, north_face, below_face, above_face)


def neighbours(padded, face_list):
    west_face, east_face, south_face, north_face, below_face, above_face = face_list
    summed = west_face * padded[..., :-2, 1:-1, 1:-1] + east_face * padded[..., 2:, 1:-1, 1:-1]
    summed = (
        summed
        + south_face * padded[..., 1:-1, :-2, 1:-1]
        + north_face * padded[..., 1:-1, 2:, 1:-1]
    )
    summed = (
        summed
        + below_face * padded[..., 1:-1, 1:-1, :-2]
        + above_face * padded[..., 1:-1, 1:-1, 2:]
    )
    return summed


def diagonal_of(face_list, shift_list, capacity):
    west_face, east_face, south_face, north_face, below_face, above_face = face_list
    summed = west_face + east_face + (south_face + north_face) + (below_face + above_face)
    return summed[None, None] + shift_list[:, None, None, None, None] * capacity[None, None]


def chebyshev(source, face_list, diagonal, padder, tie, anchor_of):
    center = 0.5 * (UPPER_BOUND + LOWER_BOUND)
    spread = 0.5 * (UPPER_BOUND - LOWER_BOUND)
    ratio_value = center / spread
    reciprocal = 1.0 / diagonal
    solution = jnp.zeros_like(source)
    remainder = source
    weight_old = 1.0 / ratio_value
    direction = reciprocal * remainder / center
    for sweep_index in range(SWEEPS):
        solution = solution + direction
        if sweep_index + 1 < SWEEPS:
            if sweep_index == 0:
                tie, direction = lax.optimization_barrier((tie, direction))
            padded = padder(direction)
            if sweep_index == 0:
                anchor, padded = lax.optimization_barrier((anchor_of(tie), padded))
            applied = diagonal * direction - neighbours(padded, face_list)
            remainder = remainder - applied
            weight_new = 1.0 / (2.0 * ratio_value - weight_old)
            direction = weight_new * weight_old * direction + 2.0 * weight_new / spread * (
                reciprocal * remainder
            )
            weight_old = weight_new
    return solution, anchor


def products(left_side, right_side):
    return lax.dot_general(
        left_side, right_side, (((1,), (1,)), ((), ())), precision=lax.Precision.HIGHEST
    )


def matmul(left_side, right_side):
    return jnp.dot(left_side, right_side, precision=lax.Precision.HIGHEST)


def local(labels, conductance, capacity_table, shift_values, prior_basis):
    groups = lax.axis_size("shift")
    shifts_all = shift_values.shape[0]
    per_device = shifts_all // groups
    new_count = shifts_all * COLS
    basis_count = prior_basis.shape[0]
    slab_x = prior_basis.shape[1]
    quarter = prior_basis.shape[2]
    depth = prior_basis.shape[3]
    flat_basis = prior_basis.reshape(basis_count, slab_x * quarter * depth)
    cell_weight = 1.0 / (slab_x * quarter * depth * groups * lax.axis_size("space"))
    tail_columns = prior_basis[basis_count - new_count :]
    conduct = lookup(labels, conductance)
    capacity = lookup(labels, capacity_table)
    rimmed = padded_2(conduct, (("space", 0),), 1)
    face_list = conductances(conduct, jnp.pad(rimmed, ((0, 0), (1, 1), (1, 1))))
    shift_list = lax.dynamic_slice_in_dim(
        shift_values, lax.axis_index("shift") * per_device, per_device, 0
    )
    diagonal = diagonal_of(face_list, shift_list, capacity)
    starting = lax.all_to_all(tail_columns, "shift", split_axis=0, concat_axis=2, tiled=True)
    full_y = starting.shape[2]
    source = starting.reshape(per_device, COLS, slab_x, full_y, depth) * capacity[None, None]

    def padder(field):
        widened = padded_2(field, (("space", 2),), 1)
        return jnp.pad(widened, ((0, 0), (0, 0), (0, 0), (1, 1), (1, 1)))

    half = basis_count // 2

    def gram_of(basis):
        return pack_symmetric(products(basis, basis), half)

    fields, packed = chebyshev(source, face_list, diagonal, padder, flat_basis, gram_of)
    pieces = [
        lax.all_to_all(fields[p], "shift", split_axis=2, concat_axis=0, tiled=True).reshape(
            groups, COLS, slab_x * quarter * depth
        )
        for p in range(per_device)
    ]
    onto_basis = [
        products(piece.reshape(groups * COLS, -1), flat_basis).reshape(groups, COLS, basis_count)
        for piece in pieces
    ]
    columns = jnp.stack(pieces, axis=1).reshape(new_count, slab_x * quarter * depth)
    onto_basis = jnp.stack(onto_basis, axis=1).reshape(new_count, basis_count)
    own = jnp.concatenate([onto_basis, products(columns, columns)], axis=1)
    total = allsum(jnp.concatenate([own.reshape(-1, half), packed], axis=0), (3, 6)) * cell_weight
    sums = total[: own.size // half].reshape(own.shape)
    basis_gram = unpack_symmetric(total[own.size // half :], half)
    first_proj = sums[:, :basis_count]
    second_proj = first_proj - matmul(first_proj, basis_gram)
    coefficients = first_proj + second_proj
    gram_matrix = (
        sums[:, basis_count:]
        - products(coefficients, first_proj)
        - products(first_proj, coefficients)
        + products(matmul(coefficients, basis_gram), coefficients)
    )
    factor = jnp.linalg.cholesky(gram_matrix)
    inverse = lax.linalg.triangular_solve(
        factor, jnp.eye(new_count, dtype=factor.dtype), left_side=True, lower=True
    )
    orthonormal = matmul(inverse, columns) - matmul(matmul(inverse, coefficients), flat_basis)
    new_block = orthonormal.reshape(shifts_all, COLS, slab_x, quarter, depth)
    return (new_block, coefficients, factor)


def solution(mesh):
    in_specs = (P("space", None, None), P(), P(), P(), P(None, "space", "shift", None))
    out_specs = (P(None, None, "space", "shift", None), P(), P())
    return jax.shard_map(local, mesh=mesh, in_specs=in_specs, out_specs=out_specs, check_vma=False)
```

```python
import jax
import jax.numpy as jnp
from jax import lax
from jax.sharding import PartitionSpec as P

COLS = 8
SWEEPS = 4


LOWER_BOUND = 0.1
UPPER_BOUND = 2.0


def padded_2(cells, sides, width):
    for axis, dim in sides:
        count = lax.axis_size(axis)
        ends = count - 1
        head = lax.slice_in_dim(cells, 0, width, axis=dim)
        tail = lax.slice_in_dim(cells, cells.shape[dim] - width, cells.shape[dim], axis=dim)
        cells = jnp.concatenate(
            [
                lax.ppermute(tail, axis, [(i, (i + 1) % count) for i in range(ends)]),
                cells,
                lax.ppermute(head, axis, [((i + 1) % count, i) for i in range(ends)]),
            ],
            axis=dim,
        )
    return cells


def exchange(value, axes, total, mask):
    return lax.ppermute(value, axes, [(i, i ^ mask) for i in range(total)])


def allsum(value, split_bits=()):
    axes = ("shift", "space")
    total = lax.axis_size("shift") * lax.axis_size("space")
    if total & (total - 1):
        return lax.psum(value, axes)
    bits = [bit for bit in range(total.bit_length() - 1) if bit not in split_bits]
    split_bits = [bit for bit in split_bits if (1 << bit) < total]
    rows = value.shape[0]
    parts = 1 << len(split_bits)
    padded_rows = -(-rows // parts) * parts
    value = jnp.pad(value, ((0, padded_rows - rows),) + ((0, 0),) * (value.ndim - 1))
    me = lax.axis_index("shift") * lax.axis_size("space") + lax.axis_index("space")
    for bit in split_bits:
        side = (me >> bit) & 1
        halves = value.reshape((2, value.shape[0] // 2) + value.shape[1:])
        keep = lax.dynamic_index_in_dim(halves, side, 0, keepdims=False)
        give = lax.dynamic_index_in_dim(halves, 1 - side, 0, keepdims=False)
        value = keep + exchange(give, axes, total, 1 << bit)
    for bit in bits:
        value = value + exchange(value, axes, total, 1 << bit)
    for bit in reversed(split_bits):
        side = (me >> bit) & 1
        other = exchange(value, axes, total, 1 << bit)
        value = jnp.where(
            side == 0,
            jnp.concatenate([value, other], axis=0),
            jnp.concatenate([other, value], axis=0),
        )
    return value[:rows]


def pack_symmetric(full, half):
    row = lax.broadcasted_iota(jnp.int32, (half, half), 0)
    col = lax.broadcasted_iota(jnp.int32, (half, half), 1)
    corner = jnp.where(row > col, full[:half, :half], full[half:, half:])
    return jnp.concatenate([full[:half, half:], corner, jnp.diagonal(full[:half, :half])[None]], axis=0)


def unpack_symmetric(packed, half):
    row = lax.broadcasted_iota(jnp.int32, (half, half), 0)
    col = lax.broadcasted_iota(jnp.int32, (half, half), 1)
    upper = packed[:half]
    corner = packed[half : 2 * half]
    first = jnp.where(row > col, corner, corner.T)
    first = jnp.where(row == col, packed[2 * half][None, :], first)
    second = jnp.where(row < col, corner, corner.T)
    return jnp.concatenate(
        [jnp.concatenate([first, upper], axis=1), jnp.concatenate([upper.T, second], axis=1)], axis=0
    )


def lookup(labels, table):
    materials = jnp.arange(table.shape[0], dtype=jnp.int32)
    onehot = (labels[None] == materials[:, None, None, None]).astype(jnp.float32)
    return jnp.sum(onehot * table[:, None, None, None], axis=0)


def conductances(conduct, padded):
    west_face = 0.5 * (conduct + padded[:-2, 1:-1, 1:-1])
    east_face = 0.5 * (conduct + padded[2:, 1:-1, 1:-1])
    south_face = 0.5 * (conduct + padded[1:-1, :-2, 1:-1])
    north_face = 0.5 * (conduct + padded[1:-1, 2:, 1:-1])
    below_face = 0.5 * (conduct + padded[1:-1, 1:-1, :-2])
    above_face = 0.5 * (conduct + padded[1:-1, 1:-1, 2:])
    return (west_face, east_face, south_face, north_face, below_face, above_face)


def neighbours(padded, face_list):
    west_face, east_face, south_face, north_face, below_face, above_face = face_list
    summed = west_face * padded[..., :-2, 1:-1, 1:-1] + east_face * padded[..., 2:, 1:-1, 1:-1]
    summed = (
        summed
        + south_face * padded[..., 1:-1, :-2, 1:-1]
        + north_face * padded[..., 1:-1, 2:, 1:-1]
    )
    summed = (
        summed
        + below_face * padded[..., 1:-1, 1:-1, :-2]
        + above_face * padded[..., 1:-1, 1:-1, 2:]
    )
    return summed


def diagonal_of(face_list, shift_list, capacity):
    west_face, east_face, south_face, north_face, below_face, above_face = face_list
    summed = west_face + east_face + (south_face + north_face) + (below_face + above_face)
    return summed[None, None] + shift_list[:, None, None, None, None] * capacity[None, None]


def chebyshev(source, face_list, diagonal, padder, tie, anchor_of):
    center = 0.5 * (UPPER_BOUND + LOWER_BOUND)
    spread = 0.5 * (UPPER_BOUND - LOWER_BOUND)
    ratio_value = center / spread
    reciprocal = 1.0 / diagonal
    solution = jnp.zeros_like(source)
    remainder = source
    weight_old = 1.0 / ratio_value
    direction = reciprocal * remainder / center
    for sweep_index in range(SWEEPS):
        solution = solution + direction
        if sweep_index + 1 < SWEEPS:
            if sweep_index == 0:
                tie, direction = lax.optimization_barrier((tie, direction))
            padded = padder(direction)
            if sweep_index == 0:
                anchor, padded = lax.optimization_barrier((anchor_of(tie), padded))
            applied = diagonal * direction - neighbours(padded, face_list)
            remainder = remainder - applied
            weight_new = 1.0 / (2.0 * ratio_value - weight_old)
            direction = weight_new * weight_old * direction + 2.0 * weight_new / spread * (
                reciprocal * remainder
            )
            weight_old = weight_new
    return solution, anchor


def products(left_side, right_side):
    return lax.dot_general(
        left_side, right_side, (((1,), (1,)), ((), ())), precision=lax.Precision.HIGHEST
    )


def matmul(left_side, right_side):
    return jnp.dot(left_side, right_side, precision=lax.Precision.HIGHEST)


def local(labels, conductance, capacity_table, shift_values, prior_basis):
    groups = lax.axis_size("shift")
    shifts_all = shift_values.shape[0]
    per_device = shifts_all // groups
    new_count = shifts_all * COLS
    basis_count = prior_basis.shape[0]
    slab_x = prior_basis.shape[1]
    quarter = prior_basis.shape[2]
    depth = prior_basis.shape[3]
    flat_basis = prior_basis.reshape(basis_count, slab_x * quarter * depth)
    cell_weight = 1.0 / (slab_x * quarter * depth * groups * lax.axis_size("space"))
    tail_columns = prior_basis[basis_count - new_count :]
    conduct = lookup(labels, conductance)
    capacity = lookup(labels, capacity_table)
    rimmed = padded_2(conduct, (("space", 0),), 1)
    face_list = conductances(conduct, jnp.pad(rimmed, ((0, 0), (1, 1), (1, 1))))
    shift_list = lax.dynamic_slice_in_dim(
        shift_values, lax.axis_index("shift") * per_device, per_device, 0
    )
    diagonal = diagonal_of(face_list, shift_list, capacity)
    starting = lax.all_to_all(tail_columns, "shift", split_axis=0, concat_axis=2, tiled=True)
    full_y = starting.shape[2]
    source = starting.reshape(per_device, COLS, slab_x, full_y, depth) * capacity[None, None]

    def padder(field):
        widened = padded_2(field, (("space", 2),), 1)
        return jnp.pad(widened, ((0, 0), (0, 0), (0, 0), (1, 1), (1, 1)))

    half = basis_count // 2

    def gram_of(basis):
        return pack_symmetric(products(basis, basis), half)

    fields, packed = chebyshev(source, face_list, diagonal, padder, flat_basis, gram_of)
    merged = fields.reshape(per_device * COLS, slab_x, full_y, depth)
    regrouped = lax.all_to_all(merged, "shift", split_axis=2, concat_axis=0, tiled=True)
    columns = regrouped.reshape(new_count, slab_x * quarter * depth)
    own = jnp.concatenate([products(columns, flat_basis), products(columns, columns)], axis=1)
    total = allsum(jnp.concatenate([own.reshape(-1, half), packed], axis=0), (7, 3, 6)) * cell_weight
    sums = total[: own.size // half].reshape(own.shape)
    basis_gram = unpack_symmetric(total[own.size // half :], half)
    first_proj = sums[:, :basis_count]
    second_proj = first_proj - matmul(first_proj, basis_gram)
    coefficients = first_proj + second_proj
    gram_matrix = (
        sums[:, basis_count:]
        - products(coefficients, first_proj)
        - products(first_proj, coefficients)
        + products(matmul(coefficients, basis_gram), coefficients)
    )
    factor = jnp.linalg.cholesky(gram_matrix)
    inverse = lax.linalg.triangular_solve(
        factor, jnp.eye(new_count, dtype=factor.dtype), left_side=True, lower=True
    )
    orthonormal = matmul(inverse, columns) - matmul(matmul(inverse, coefficients), flat_basis)
    new_block = orthonormal.reshape(shifts_all, COLS, slab_x, quarter, depth)
    return (new_block, coefficients, factor)


def solution(mesh):
    in_specs = (P("space", None, None), P(), P(), P(), P(None, "space", "shift", None))
    out_specs = (P(None, None, "space", "shift", None), P(), P())
    return jax.shard_map(local, mesh=mesh, in_specs=in_specs, out_specs=out_specs, check_vma=False)
```

```python
import jax
import jax.numpy as jnp
from jax import lax
from jax.sharding import PartitionSpec as P

COLS = 8
SWEEPS = 4


LOWER_BOUND = 0.1
UPPER_BOUND = 2.0


def padded_2(cells, sides, width):
    for axis, dim in sides:
        count = lax.axis_size(axis)
        ends = count - 1
        head = lax.slice_in_dim(cells, 0, width, axis=dim)
        tail = lax.slice_in_dim(cells, cells.shape[dim] - width, cells.shape[dim], axis=dim)
        cells = jnp.concatenate(
            [
                lax.ppermute(tail, axis, [(i, (i + 1) % count) for i in range(ends)]),
                cells,
                lax.ppermute(head, axis, [((i + 1) % count, i) for i in range(ends)]),
            ],
            axis=dim,
        )
    return cells


def exchange(value, axes, total, mask):
    return lax.ppermute(value, axes, [(i, i ^ mask) for i in range(total)])


def allsum(value, split_bits=()):
    axes = ("shift", "space")
    total = lax.axis_size("shift") * lax.axis_size("space")
    if total & (total - 1):
        return lax.psum(value, axes)
    bits = [bit for bit in range(total.bit_length() - 1) if bit not in split_bits]
    split_bits = [bit for bit in split_bits if (1 << bit) < total]
    rows = value.shape[0]
    parts = 1 << len(split_bits)
    padded_rows = -(-rows // parts) * parts
    value = jnp.pad(value, ((0, padded_rows - rows),) + ((0, 0),) * (value.ndim - 1))
    me = lax.axis_index("shift") * lax.axis_size("space") + lax.axis_index("space")
    for bit in split_bits:
        side = (me >> bit) & 1
        halves = value.reshape((2, value.shape[0] // 2) + value.shape[1:])
        keep = lax.dynamic_index_in_dim(halves, side, 0, keepdims=False)
        give = lax.dynamic_index_in_dim(halves, 1 - side, 0, keepdims=False)
        value = keep + exchange(give, axes, total, 1 << bit)
    for bit in bits:
        value = value + exchange(value, axes, total, 1 << bit)
    for bit in reversed(split_bits):
        side = (me >> bit) & 1
        other = exchange(value, axes, total, 1 << bit)
        value = jnp.where(
            side == 0,
            jnp.concatenate([value, other], axis=0),
            jnp.concatenate([other, value], axis=0),
        )
    return value[:rows]


def pack_symmetric(full, half):
    row = lax.broadcasted_iota(jnp.int32, (half, half), 0)
    col = lax.broadcasted_iota(jnp.int32, (half, half), 1)
    corner = jnp.where(row > col, full[:half, :half], full[half:, half:])
    return jnp.concatenate([full[:half, half:], corner, jnp.diagonal(full[:half, :half])[None]], axis=0)


def unpack_symmetric(packed, half):
    row = lax.broadcasted_iota(jnp.int32, (half, half), 0)
    col = lax.broadcasted_iota(jnp.int32, (half, half), 1)
    upper = packed[:half]
    corner = packed[half : 2 * half]
    first = jnp.where(row > col, corner, corner.T)
    first = jnp.where(row == col, packed[2 * half][None, :], first)
    second = jnp.where(row < col, corner, corner.T)
    return jnp.concatenate(
        [jnp.concatenate([first, upper], axis=1), jnp.concatenate([upper.T, second], axis=1)], axis=0
    )


def lookup(labels, table):
    materials = jnp.arange(table.shape[0], dtype=jnp.int32)
    onehot = (labels[None] == materials[:, None, None, None]).astype(jnp.float32)
    return jnp.sum(onehot * table[:, None, None, None], axis=0)


def conductances(conduct, padded):
    west_face = 0.5 * (conduct + padded[:-2, 1:-1, 1:-1])
    east_face = 0.5 * (conduct + padded[2:, 1:-1, 1:-1])
    south_face = 0.5 * (conduct + padded[1:-1, :-2, 1:-1])
    north_face = 0.5 * (conduct + padded[1:-1, 2:, 1:-1])
    below_face = 0.5 * (conduct + padded[1:-1, 1:-1, :-2])
    above_face = 0.5 * (conduct + padded[1:-1, 1:-1, 2:])
    return (west_face, east_face, south_face, north_face, below_face, above_face)


def neighbours(padded, face_list):
    west_face, east_face, south_face, north_face, below_face, above_face = face_list
    summed = west_face * padded[..., :-2, 1:-1, 1:-1] + east_face * padded[..., 2:, 1:-1, 1:-1]
    summed = (
        summed
        + south_face * padded[..., 1:-1, :-2, 1:-1]
        + north_face * padded[..., 1:-1, 2:, 1:-1]
    )
    summed = (
        summed
        + below_face * padded[..., 1:-1, 1:-1, :-2]
        + above_face * padded[..., 1:-1, 1:-1, 2:]
    )
    return summed


def diagonal_of(face_list, shift_list, capacity):
    west_face, east_face, south_face, north_face, below_face, above_face = face_list
    summed = west_face + east_face + (south_face + north_face) + (below_face + above_face)
    return summed[None, None] + shift_list[:, None, None, None, None] * capacity[None, None]


def chebyshev(source, face_list, diagonal, padder, tie, anchor_of):
    center = 0.5 * (UPPER_BOUND + LOWER_BOUND)
    spread = 0.5 * (UPPER_BOUND - LOWER_BOUND)
    ratio_value = center / spread
    reciprocal = 1.0 / diagonal
    solution = jnp.zeros_like(source)
    remainder = source
    weight_old = 1.0 / ratio_value
    direction = reciprocal * remainder / center
    for sweep_index in range(SWEEPS):
        solution = solution + direction
        if sweep_index + 1 < SWEEPS:
            if sweep_index == 0:
                tie, direction = lax.optimization_barrier((tie, direction))
            padded = padder(direction)
            if sweep_index == 0:
                anchor, padded = lax.optimization_barrier((anchor_of(tie), padded))
            applied = diagonal * direction - neighbours(padded, face_list)
            remainder = remainder - applied
            weight_new = 1.0 / (2.0 * ratio_value - weight_old)
            direction = weight_new * weight_old * direction + 2.0 * weight_new / spread * (
                reciprocal * remainder
            )
            weight_old = weight_new
    return solution, anchor


def products(left_side, right_side):
    return lax.dot_general(
        left_side, right_side, (((1,), (1,)), ((), ())), precision=lax.Precision.HIGHEST
    )


def matmul(left_side, right_side):
    return jnp.dot(left_side, right_side, precision=lax.Precision.HIGHEST)


def local(labels, conductance, capacity_table, shift_values, prior_basis):
    groups = lax.axis_size("shift")
    shifts_all = shift_values.shape[0]
    per_device = shifts_all // groups
    new_count = shifts_all * COLS
    basis_count = prior_basis.shape[0]
    slab_x = prior_basis.shape[1]
    quarter = prior_basis.shape[2]
    depth = prior_basis.shape[3]
    flat_basis = prior_basis.reshape(basis_count, slab_x * quarter * depth)
    cell_weight = 1.0 / (slab_x * quarter * depth * groups * lax.axis_size("space"))
    tail_columns = prior_basis[basis_count - new_count :]
    conduct = lookup(labels, conductance)
    capacity = lookup(labels, capacity_table)
    rimmed = padded_2(conduct, (("space", 0),), 1)
    face_list = conductances(conduct, jnp.pad(rimmed, ((0, 0), (1, 1), (1, 1))))
    shift_list = lax.dynamic_slice_in_dim(
        shift_values, lax.axis_index("shift") * per_device, per_device, 0
    )
    diagonal = diagonal_of(face_list, shift_list, capacity)
    starting = lax.all_to_all(tail_columns, "shift", split_axis=0, concat_axis=2, tiled=True)
    full_y = starting.shape[2]
    source = starting.reshape(per_device, COLS, slab_x, full_y, depth) * capacity[None, None]

    def padder(field):
        widened = padded_2(field, (("space", 2),), 1)
        return jnp.pad(widened, ((0, 0), (0, 0), (0, 0), (1, 1), (1, 1)))

    half = basis_count // 2

    def gram_of(basis):
        return pack_symmetric(products(basis, basis), half)

    fields, packed = chebyshev(source, face_list, diagonal, padder, flat_basis, gram_of)
    merged = fields.reshape(per_device * COLS, slab_x, full_y, depth)
    regrouped = lax.all_to_all(merged, "shift", split_axis=2, concat_axis=0, tiled=True)
    columns = regrouped.reshape(new_count, slab_x * quarter * depth)
    own = jnp.concatenate([products(columns, flat_basis), products(columns, columns)], axis=1)
    total = allsum(jnp.concatenate([own.reshape(-1, half), packed], axis=0), (7, 3, 6)) * cell_weight
    sums = total[: own.size // half].reshape(own.shape)
    basis_gram = unpack_symmetric(total[own.size // half :], half)
    first_proj = sums[:, :basis_count]
    second_proj = first_proj - matmul(first_proj, basis_gram)
    coefficients = first_proj + second_proj
    gram_matrix = (
        sums[:, basis_count:]
        - products(coefficients, first_proj)
        - products(first_proj, coefficients)
        + products(matmul(coefficients, basis_gram), coefficients)
    )
    factor = lax.linalg.cholesky(gram_matrix, symmetrize_input=False)
    inverse = lax.linalg.triangular_solve(
        factor, jnp.eye(new_count, dtype=factor.dtype), left_side=True, lower=True
    )
    orthonormal = matmul(inverse, columns) - matmul(matmul(inverse, coefficients), flat_basis)
    new_block = orthonormal.reshape(shifts_all, COLS, slab_x, quarter, depth)
    return (new_block, coefficients, factor)


def solution(mesh):
    in_specs = (P("space", None, None), P(), P(), P(), P(None, "space", "shift", None))
    out_specs = (P(None, None, "space", "shift", None), P(), P())
    return jax.shard_map(local, mesh=mesh, in_specs=in_specs, out_specs=out_specs, check_vma=False)
```
